256 devices in a mesh: rep: 4 (over x), gx: 8 (over z), gy: 8 (over y, core).
Axes of the slice: x: 4, y: 4, z: 8, core: 2. Of those that a mesh axis runs over, the one named last changes fastest.
Arguments:
- features: bfloat16 [4, 8, 8, 512, 128], P('rep', 'gx', 'gy'), may hold values from -6 to 6
- species: int32 [4, 8, 8, 512], P('rep', 'gx', 'gy'), may hold values from 0 to 2
- atom_nbr: int32 [4, 8, 8, 512, 32], P('rep', 'gx', 'gy'), may hold values from 0 to 1535, as said below
- atom_nbr_count: int32 [4, 8, 8, 512], P('rep', 'gx', 'gy'), may hold values from 16 to 32
- atom_dist: float32 [4, 8, 8, 512, 32], P('rep', 'gx', 'gy'), may hold values from 0.8 to 3.9
- send_list: int32 [4, 8, 8, 8, 128], P('rep', 'gx', 'gy'), may hold values from 0 to 511
- probe_nbr: int32 [4, 8, 8, 1024, 32], P('rep', 'gx', 'gy'), may hold values from 0 to 1535, as said below
- probe_dist: float32 [4, 8, 8, 1024, 32], P('rep', 'gx', 'gy'), may hold values from 0.3 to 3.9
- probe_count: int32 [4, 8, 8], P('rep', 'gx', 'gy'), may hold values from 128 to 1024, as said below
- d_density: float32 [4, 8, 8, 1024], P('rep', 'gx', 'gy'), may hold values from -0.03 to 0.03
- species_gain: float32 [3, 128], replicated, may hold values from 0.1 to 1.9
- proj_input: bfloat16 [128, 128], replicated, may hold values from -0.5 to 0.5
- atom_radial: bfloat16 [20, 128], replicated, may hold values from -4 to 4
- atom_filter: bfloat16 [128, 128], replicated, may hold values from -0.5 to 0.5
- mix_first: bfloat16 [128, 128], replicated, may hold values from -0.5 to 0.5
- mix_second: bfloat16 [128, 128], replicated, may hold values from -0.5 to 0.5
- proj_probe: bfloat16 [128, 128], replicated, may hold values from -0.5 to 0.5
- probe_radial: bfloat16 [20, 128], replicated, may hold values from -4 to 4
- probe_filter: bfloat16 [128, 128], replicated, may hold values from -0.5 to 0.5
- read_weight: bfloat16 [128, 128], replicated, may hold values from -0.5 to 0.5
- final_weight: float32 [128], replicated, may hold values from -0.5 to 0.5
Outputs:
- d_features: float32 [4, 8, 8, 512, 128], P('rep', 'gx', 'gy')
- grad_square: float32 [7, 128, 128], replicated
- grad_radial: float32 [2, 20, 128], replicated
- grad_vector: float32 [4, 128], replicated
The draws below stay inside these ranges and needn't reach their ends.
Inputs may be any that keep to these rules, and one draw needn't show every extreme that they name: `atom_nbr`: entries below 512 name the tile's own atoms; entry 512 + k * 128 + g names row g of ghost block k. About a quarter of the entries name ghost rows. `probe_nbr`: same layout as atom_nbr. About a quarter of the entries name ghost rows. `probe_count`: equal to 1024 on at least one tile of every draw.
All inputs are finite; a program needn't handle non-finite values.
Results may differ from the reference program's by a relative error of at most 0.014.
Values may be sent and summed in bfloat16 or wider, within the bound.
No kernel may reach another device: no remote copies, remote signals or barrier semaphores. Data moves between devices by JAX's collectives and lax.ppermute only.
A program may use at most 64 MiB of HBM per device.

```python
import math
import jax
import jax.numpy as jnp
from jax import lax

F = 128
RADIAL = 20
KINDS = 3
ATOM_NBRS = 32
PROBE_NBRS = 32
ATOMS_DEV = 512
PROBES_DEV = 1024
GHOSTS = 128
SNAPS = 4
TILES_X = 8
TILES_Y = 8


def neighbour_rows(key, shape):
    keys = jax.random.split(key, 4)
    local = jax.random.randint(keys[0], shape, 0, ATOMS_DEV)
    block_index = jax.random.randint(keys[1], shape, 0, 8)
    ghost_row = jax.random.randint(keys[2], shape, 0, GHOSTS)
    selector = jax.random.randint(keys[3], shape, 0, 4)
    return jnp.where(selector == 0, ATOMS_DEV + block_index * GHOSTS + ghost_row, local).astype(jnp.int32)


def draw_atom_nbr(key, part):
    return neighbour_rows(jax.random.fold_in(key, 11), (SNAPS, TILES_X, TILES_Y, ATOMS_DEV, ATOM_NBRS))


def draw_probe_nbr(key, part):
    return neighbour_rows(jax.random.fold_in(key, 23), (SNAPS, TILES_X, TILES_Y, PROBES_DEV, PROBE_NBRS))


def draw_probe_count(key, part):
    keys = jax.random.split(jax.random.fold_in(key, 37), 2)
    shape = (SNAPS, TILES_X, TILES_Y)
    partial_load = jax.random.randint(keys[0], shape, PROBES_DEV // 8, PROBES_DEV // 2 + 1)
    selector = jax.random.randint(keys[1], shape, 0, 8)
    first_tile = (jnp.arange(SNAPS * TILES_X * TILES_Y, dtype=jnp.int32) == 0).reshape(shape)
    return jnp.where((selector == 0) | first_tile, PROBES_DEV, partial_load).astype(jnp.int32)


def touch_ends(drawn, key, low, high):
    longest = drawn.shape.index(max(drawn.shape))
    spots = []
    for shift in (0, 1):
        where = [jax.random.randint(jax.random.fold_in(key, axis), (), 0, length) for axis, length in enumerate(drawn.shape)]
        where[longest] = (where[longest] + shift) % drawn.shape[longest]
        spots.append(tuple(where))
    return drawn.at[spots[0]].set(low).at[spots[1]].set(high)


def level_of(own_key, shape, cuts, low, largest):
    def one(position, parts):
        draws = jax.random.uniform(jax.random.fold_in(jax.random.fold_in(own_key, 6), position), (parts,), jnp.float32, low / len(cuts), largest / len(cuts))
        return jnp.repeat(jnp.exp(draws), shape[position] // parts).reshape((-1,) + (1,) * (len(shape) - position - 1))

    factor_of = one(*cuts[0])
    for cut in cuts[1:]:
        factor_of = factor_of * one(*cut)
    return factor_of


def centred(rng, extent, width, bound, shards=(), kind=jnp.bfloat16):
    values = jax.random.normal(rng, extent, jnp.float32) * width
    if len(shards) > 0:
        values = level_of(rng, extent, shards, -0.22, 0.18) * values
    return jnp.clip(values, min=-bound, max=bound).astype(kind)


def setup_inputs(seed: int = 0) -> dict:
    seeds = jax.random.split(jax.random.key(seed), 22)
    return {
        "features": centred(seeds[0], (SNAPS, TILES_X, TILES_Y, ATOMS_DEV, F), 1.0, 6.0, ((0, 4), (1, 8), (2, 8))),
        "species": touch_ends(jax.random.randint(seeds[1], (SNAPS, TILES_X, TILES_Y, ATOMS_DEV), 0, KINDS), jax.random.fold_in(seeds[1], 1), 0, KINDS - 1).astype(jnp.int32),
        "atom_nbr": draw_atom_nbr(jax.random.fold_in(seeds[21], 71), 0),
        "atom_nbr_count": touch_ends(jax.random.randint(seeds[3], (SNAPS, TILES_X, TILES_Y, ATOMS_DEV), ATOM_NBRS // 2, ATOM_NBRS + 1), jax.random.fold_in(seeds[3], 1), ATOM_NBRS // 2, ATOM_NBRS).astype(jnp.int32),
        "atom_dist": jnp.clip(0.8 + 3.1000001 * jax.random.uniform(seeds[4], (SNAPS, TILES_X, TILES_Y, ATOMS_DEV, ATOM_NBRS), jnp.float32) ** level_of(seeds[4], (SNAPS, TILES_X, TILES_Y, ATOMS_DEV, ATOM_NBRS), ((0, 4), (1, 8), (2, 8)), -0.2, 0.2), 0.8, 3.9),
        "send_list": touch_ends(jax.random.randint(seeds[5], (SNAPS, TILES_X, TILES_Y, 8, GHOSTS), 0, ATOMS_DEV), jax.random.fold_in(seeds[5], 1), 0, ATOMS_DEV - 1).astype(jnp.int32),
        "probe_nbr": draw_probe_nbr(jax.random.fold_in(seeds[21], 71), 0),
        "probe_dist": jnp.clip(0.3 + 3.6000001 * jax.random.uniform(seeds[7], (SNAPS, TILES_X, TILES_Y, PROBES_DEV, PROBE_NBRS), jnp.float32) ** level_of(seeds[7], (SNAPS, TILES_X, TILES_Y, PROBES_DEV, PROBE_NBRS), ((0, 4), (1, 8), (2, 8)), -0.2, 0.2), 0.3, 3.9),
        "probe_count": draw_probe_count(jax.random.fold_in(seeds[21], 71), 0),
        "d_density": centred(seeds[9], (SNAPS, TILES_X, TILES_Y, PROBES_DEV), 0.005, 0.03, ((0, 4), (1, 8), (2, 8)), jnp.float32),
        "species_gain": jnp.clip(1.0 + 0.18 * jax.random.normal(seeds[10], (KINDS, F), jnp.float32), 0.1, 1.9),
        "proj_input": centred(seeds[11], (F, F), F ** -0.5, 0.5),
        "atom_radial": centred(seeds[12], (RADIAL, F), 2 ** -0.5, 4.0),
        "atom_filter": centred(seeds[13], (F, F), F ** -0.5, 0.5),
        "mix_first": centred(seeds[14], (F, F), F ** -0.5, 0.5),
        "mix_second": centred(seeds[15], (F, F), F ** -0.5, 0.5),
        "proj_probe": centred(seeds[16], (F, F), F ** -0.5, 0.5),
        "probe_radial": centred(seeds[17], (RADIAL, F), 2 ** -0.5, 4.0),
        "probe_filter": centred(seeds[18], (F, F), F ** -0.5, 0.5),
        "read_weight": centred(seeds[19], (F, F), F ** -0.5, 0.5),
        "final_weight": centred(seeds[20], (F,), F ** -0.5, 0.5, (), jnp.float32),
    }


cutoff_radius = 4.0
offsets = ((-1, -1), (-1, 0), (-1, 1), (0, -1), (0, 1), (1, -1), (1, 0), (1, 1))


def shifted_plus(values):
    return jax.nn.softplus(values) - math.log(2.0)


def contract_rows(former, latter):
    return lax.dot_general(former, latter, (((0,), (0,)), ((), ())), preferred_element_type=jnp.float32)


def contract_cols(former, latter):
    return lax.dot_general(former, latter, (((1,), (1,)), ((), ())), preferred_element_type=jnp.float32)


def edge_setup(indices, distances, live_mask, row_table, radial_weight, filter_weight):
    flat_dist = distances.reshape(-1)
    spacing = cutoff_radius / (radial_weight.shape[0] - 1)
    centers = jnp.arange(radial_weight.shape[0], dtype=jnp.float32) * spacing
    scaled = (flat_dist[None, :] - centers[:, None]) / spacing
    expansion = jnp.exp(-scaled * scaled).astype(jnp.bfloat16)
    pre_act = contract_rows(expansion, radial_weight)
    hidden = shifted_plus(pre_act).astype(jnp.bfloat16)
    envelope = 0.5 * (jnp.cos(math.pi * flat_dist / cutoff_radius) + 1.0) * live_mask.reshape(-1)
    filters = jnp.dot(hidden, filter_weight, preferred_element_type=jnp.float32) * envelope[:, None]
    gathered = row_table[indices.reshape(-1)].astype(jnp.float32)
    return expansion, pre_act, hidden, envelope, filters, gathered


def edge_sums(stored, slot_count):
    filters = stored[4]
    gathered = stored[5]
    terms = (gathered * filters).reshape(-1, slot_count, filters.shape[1])
    return jnp.sum(terms, axis=1)


def edge_backward(stored, indices, filter_weight, grad_message, totals):
    expansion, pre_act, hidden, envelope, filters, gathered = stored
    grad_table, grad_radial, grad_filter = totals
    feature_width = grad_message.shape[1]
    spread = jnp.broadcast_to(grad_message[:, None, :], (grad_message.shape[0], indices.shape[1], feature_width)).reshape(-1, feature_width)
    grad_table = grad_table.at[indices.reshape(-1)].add(spread * filters)
    grad_out = (spread * gathered * envelope[:, None]).astype(jnp.bfloat16)
    grad_filter = grad_filter + contract_rows(hidden, grad_out)
    grad_pre = (contract_cols(grad_out, filter_weight) * jax.nn.sigmoid(pre_act)).astype(jnp.bfloat16)
    grad_radial = grad_radial + jnp.dot(expansion, grad_pre, preferred_element_type=jnp.float32)
    return grad_table, grad_radial, grad_filter


def slot_mask(counts, slot_count):
    return (jnp.arange(slot_count, dtype=jnp.int32)[None, :] < counts[:, None]).astype(jnp.float32)


def atom_messages(indices, distances, counts, row_table, radial_weight, filter_weight):
    atom_count, slot_count = indices.shape
    block_rows = min(64, atom_count)
    pieces = (indices.reshape(-1, block_rows, slot_count), distances.reshape(-1, block_rows, slot_count), slot_mask(counts, slot_count).reshape(-1, block_rows, slot_count))

    def one_block(portion):
        stored = edge_setup(portion[0], portion[1], portion[2], row_table, radial_weight, filter_weight)
        return edge_sums(stored, slot_count)

    return lax.map(one_block, pieces).reshape(atom_count, -1)


def atom_backward(indices, distances, counts, row_table, radial_weight, filter_weight, grad_message):
    atom_count, slot_count = indices.shape
    block_rows = min(64, atom_count)
    pieces = (indices.reshape(-1, block_rows, slot_count), distances.reshape(-1, block_rows, slot_count), slot_mask(counts, slot_count).reshape(-1, block_rows, slot_count), grad_message.reshape(-1, block_rows, grad_message.shape[1]))
    initial = (jnp.zeros(row_table.shape, jnp.float32), jnp.zeros(radial_weight.shape, jnp.float32), jnp.zeros(filter_weight.shape, jnp.float32))

    def advance(totals, portion):
        stored = edge_setup(portion[0], portion[1], portion[2], row_table, radial_weight, filter_weight)
        return edge_backward(stored, portion[0], filter_weight, portion[3], totals), None

    return lax.scan(advance, initial, pieces)[0]


def probe_block(totals, indices, distances, cotangent, row_table, probe_radial, probe_filter, read_weight, final_weight):
    grad_table, grad_radial, grad_filter, grad_read, grad_final = totals
    stored = edge_setup(indices, distances, jnp.ones(indices.shape, jnp.float32), row_table, probe_radial, probe_filter)
    packed = edge_sums(stored, indices.shape[1]).astype(jnp.bfloat16)
    read_pre = jnp.dot(packed, read_weight, preferred_element_type=jnp.float32)
    grad_final = grad_final + jnp.sum(cotangent[:, None] * shifted_plus(read_pre), axis=0)
    grad_inner = (cotangent[:, None] * final_weight[None, :] * jax.nn.sigmoid(read_pre)).astype(jnp.bfloat16)
    grad_read = grad_read + contract_rows(packed, grad_inner)
    grad_feats = contract_cols(grad_inner, read_weight)
    edge_totals = edge_backward(stored, indices, probe_filter, grad_feats, (grad_table, grad_radial, grad_filter))
    return edge_totals + (grad_read, grad_final)


def interaction_head(atom_feats, kinds, species_gain, proj_input):
    onehot = (kinds[:, None] == jnp.arange(species_gain.shape[0], dtype=jnp.int32)[None, :]).astype(jnp.float32)
    gains = jnp.dot(onehot, species_gain, precision=lax.Precision.HIGHEST)
    scaled = (atom_feats.astype(jnp.float32) * gains).astype(jnp.bfloat16)
    projected = jnp.dot(scaled, proj_input, preferred_element_type=jnp.float32).astype(jnp.bfloat16)
    return onehot, gains, scaled, projected


def interaction_tail(atom_feats, message, mix_first, mix_second, proj_probe):
    packed_msg = message.astype(jnp.bfloat16)
    mix_pre = jnp.dot(packed_msg, mix_first, preferred_element_type=jnp.float32)
    activation = shifted_plus(mix_pre).astype(jnp.bfloat16)
    updated = (atom_feats.astype(jnp.float32) + jnp.dot(activation, mix_second, preferred_element_type=jnp.float32)).astype(jnp.bfloat16)
    probe_proj = jnp.dot(updated, proj_probe, preferred_element_type=jnp.float32).astype(jnp.bfloat16)
    return packed_msg, mix_pre, activation, updated, probe_proj


def tail_backward(grad_proj, packed_msg, mix_pre, activation, updated, mix_first, mix_second, proj_probe):
    grad_packed = grad_proj.astype(jnp.bfloat16)
    grad_proj_probe = contract_rows(updated, grad_packed)
    grad_updated = contract_cols(grad_packed, proj_probe)
    grad_upd_packed = grad_updated.astype(jnp.bfloat16)
    grad_mix_second = contract_rows(activation, grad_upd_packed)
    grad_mix_pre = (contract_cols(grad_upd_packed, mix_second) * jax.nn.sigmoid(mix_pre)).astype(jnp.bfloat16)
    grad_mix_first = contract_rows(packed_msg, grad_mix_pre)
    grad_message = contract_cols(grad_mix_pre, mix_first)
    return grad_updated, grad_message, grad_proj_probe, grad_mix_second, grad_mix_first


def head_backward(grad_proj, grad_updated, atom_feats, onehot, gains, scaled, proj_input):
    grad_packed = grad_proj.astype(jnp.bfloat16)
    grad_proj_input = contract_rows(scaled, grad_packed)
    grad_scaled = contract_cols(grad_packed, proj_input)
    d_features = grad_updated + grad_scaled * gains
    grad_gain = lax.dot_general(onehot, grad_scaled * atom_feats.astype(jnp.float32), (((0,), (0,)), ((), ())), precision=lax.Precision.HIGHEST)
    return d_features, grad_proj_input, grad_gain


def pick_rows(row_table, send_rows):
    return row_table[send_rows]


def add_rows(base, send_rows, returned):
    return base.at[send_rows.reshape(-1)].add(returned.reshape(-1, returned.shape[-1]))


def route(blocks):
    moved = []
    for offset_index in range(8):
        step_x, step_y = offsets[offset_index]
        moved.append(jnp.roll(blocks[:, :, :, 7 - offset_index], (-step_x, -step_y), axis=(1, 2)))
    return jnp.stack(moved, axis=3)


def reference(features, species, atom_nbr, atom_nbr_count, atom_dist, send_list, probe_nbr, probe_dist, probe_count, d_density, species_gain, proj_input, atom_radial, atom_filter, mix_first, mix_second, proj_probe, probe_radial, probe_filter, read_weight, final_weight):
    grid_shape = features.shape[:3]
    tile_count = grid_shape[0] * grid_shape[1] * grid_shape[2]
    atom_count = features.shape[3]

    def tiles_flat(values):
        return values.reshape((tile_count,) + values.shape[3:])

    def tiles_grid(values):
        return values.reshape(grid_shape + values.shape[1:])

    tile_feats = tiles_flat(features)
    tile_send = tiles_flat(send_list)

    def with_ghosts(projected):
        ghosts = tiles_flat(route(tiles_grid(jax.vmap(pick_rows)(projected, tile_send))))
        return jnp.concatenate([projected, ghosts.reshape(tile_count, -1, projected.shape[-1])], axis=1)

    def returned_sum(grad_table):
        ghost_part = grad_table[:, atom_count:].reshape(tile_send.shape + (grad_table.shape[-1],))
        returned = tiles_flat(route(tiles_grid(ghost_part)))
        return jax.vmap(add_rows)(grad_table[:, :atom_count], tile_send, returned)

    onehot, gains, scaled, projected = jax.vmap(interaction_head, in_axes=(0, 0, None, None))(tile_feats, tiles_flat(species), species_gain, proj_input)
    row_table = with_ghosts(projected)
    tile_nbr = tiles_flat(atom_nbr)
    tile_dist = tiles_flat(atom_dist)
    tile_counts = tiles_flat(atom_nbr_count)

    def tile_messages(portion):
        return atom_messages(portion[0], portion[1], portion[2], portion[3], atom_radial, atom_filter)

    message = lax.map(tile_messages, (tile_nbr, tile_dist, tile_counts, row_table))
    packed_msg, mix_pre, activation, updated, probe_proj = jax.vmap(interaction_tail, in_axes=(0, 0, None, None, None))(tile_feats, message, mix_first, mix_second, proj_probe)
    probe_table = with_ghosts(probe_proj)
    probe_total = probe_nbr.shape[3]
    positions = jnp.arange(probe_total, dtype=jnp.int32)
    cotangents = tiles_flat(d_density) * (positions[None, :] < tiles_flat(probe_count)[:, None]).astype(jnp.float32)

    def tile_probes(portion):
        indices, distances, cotangent, table_rows = portion
        block_rows = min(64, probe_total)
        pieces = (indices.reshape(-1, block_rows, indices.shape[1]), distances.reshape(-1, block_rows, distances.shape[1]), cotangent.reshape(-1, block_rows))
        initial = (jnp.zeros(table_rows.shape, jnp.float32), jnp.zeros(probe_radial.shape, jnp.float32), jnp.zeros(probe_filter.shape, jnp.float32), jnp.zeros(read_weight.shape, jnp.float32), jnp.zeros(final_weight.shape, jnp.float32))

        def advance(totals, section):
            return probe_block(totals, section[0], section[1], section[2], table_rows, probe_radial, probe_filter, read_weight, final_weight), None

        return lax.scan(advance, initial, pieces)[0]

    grad_ptable, grad_pradial, grad_pfilter, grad_read, grad_final = lax.map(tile_probes, (tiles_flat(probe_nbr), tiles_flat(probe_dist), cotangents, probe_table))
    grad_q = returned_sum(grad_ptable)
    grad_updated, grad_message, grad_proj_probe, grad_mix_second, grad_mix_first = jax.vmap(tail_backward, in_axes=(0, 0, 0, 0, 0, None, None, None))(grad_q, packed_msg, mix_pre, activation, updated, mix_first, mix_second, proj_probe)

    def tile_atom_grads(portion):
        return atom_backward(portion[0], portion[1], portion[2], portion[3], atom_radial, atom_filter, portion[4])

    grad_atable, grad_aradial, grad_afilter = lax.map(tile_atom_grads, (tile_nbr, tile_dist, tile_counts, row_table, grad_message))
    grad_u = returned_sum(grad_atable)
    d_features, grad_proj_input, grad_gain = jax.vmap(head_backward, in_axes=(0, 0, 0, 0, 0, 0, None))(grad_u, grad_updated, tile_feats, onehot, gains, scaled, proj_input)
    grad_square = jnp.stack([jnp.sum(grad_pfilter, axis=0), jnp.sum(grad_read, axis=0), jnp.sum(grad_afilter, axis=0), jnp.sum(grad_proj_input, axis=0), jnp.sum(grad_mix_first, axis=0), jnp.sum(grad_mix_second, axis=0), jnp.sum(grad_proj_probe, axis=0)], axis=0)
    grad_radial = jnp.stack([jnp.sum(grad_pradial, axis=0), jnp.sum(grad_aradial, axis=0)], axis=0)
    grad_vector = jnp.concatenate([jnp.sum(grad_final, axis=0)[None, :], jnp.sum(grad_gain, axis=0)], axis=0)
    return tiles_grid(d_features), grad_square, grad_radial, grad_vector
```

```python
import math

import jax
import jax.numpy as jnp
from jax import lax
from jax.sharding import PartitionSpec as P

cutoff_radius = 4.0


def with_halo(block, sides, width):
    for axis, dim in sides:
        count = lax.axis_size(axis)
        forward = [(i, i + 1) for i in range(count - 1)]
        forward.append((count - 1, 0))
        backward = [(target, source) for source, target in forward]
        low = lax.ppermute(
            lax.slice_in_dim(block, block.shape[dim] - width, None, axis=dim), axis, forward
        )
        high = lax.ppermute(lax.slice_in_dim(block, 0, width, axis=dim), axis, backward)
        block = jnp.concatenate([low, block, high], axis=dim)
    return block


def shifted_plus(values):
    return jax.nn.softplus(values) - math.log(2.0)


def contract_rows(former, latter):
    return lax.dot_general(
        former, latter, (((0,), (0,)), ((), ())), preferred_element_type=jnp.float32
    )


def contract_cols(former, latter):
    return lax.dot_general(
        former, latter, (((1,), (1,)), ((), ())), preferred_element_type=jnp.float32
    )


def one_hot_rows(indices, row_count):
    flat = indices.reshape(-1)
    return (flat[:, None] == jnp.arange(row_count, dtype=jnp.int32)[None, :]).astype(jnp.bfloat16)


def scatter_rows(selector, values):
    high = values.astype(jnp.bfloat16)
    low = (values - high.astype(jnp.float32)).astype(jnp.bfloat16)
    both = contract_rows(selector, jnp.concatenate([high, low], axis=1))
    return both[:, : values.shape[1]] + both[:, values.shape[1] :]


def edge_setup(indices, distances, live_mask, row_table, radial_weight, filter_weight):
    flat_dist = distances.reshape(-1)
    spacing = cutoff_radius / (radial_weight.shape[0] - 1)
    centers = jnp.arange(radial_weight.shape[0], dtype=jnp.float32) * spacing
    scaled = (flat_dist[None, :] - centers[:, None]) / spacing
    expansion = jnp.exp(-scaled * scaled).astype(jnp.bfloat16)
    pre_act = contract_rows(expansion, radial_weight)
    hidden = shifted_plus(pre_act).astype(jnp.bfloat16)
    envelope = 0.5 * (jnp.cos(math.pi * flat_dist / cutoff_radius) + 1.0) * live_mask.reshape(-1)
    filters = jnp.dot(hidden, filter_weight, preferred_element_type=jnp.float32) * envelope[:, None]
    selector = one_hot_rows(indices, row_table.shape[0])
    gathered = jnp.dot(selector, row_table, preferred_element_type=jnp.float32)
    return (expansion, pre_act, hidden, envelope, filters, gathered, selector)


def edge_sums(stored, slot_count):
    filters = stored[4]
    gathered = stored[5]
    terms = (gathered * filters).reshape(-1, slot_count, filters.shape[1])
    return jnp.sum(terms, axis=1)


def edge_backward(stored, indices, filter_weight, grad_message, totals):
    expansion, pre_act, hidden, envelope, filters, gathered, selector = stored
    grad_table, grad_radial, grad_filter = totals
    feature_width = grad_message.shape[1]
    spread = jnp.broadcast_to(
        grad_message[:, None, :], (grad_message.shape[0], indices.shape[1], feature_width)
    ).reshape(-1, feature_width)
    grad_table = grad_table + scatter_rows(selector, spread * filters)
    grad_out = (spread * gathered * envelope[:, None]).astype(jnp.bfloat16)
    grad_filter = grad_filter + contract_rows(hidden, grad_out)
    grad_pre = (contract_cols(grad_out, filter_weight) * jax.nn.sigmoid(pre_act)).astype(
        jnp.bfloat16
    )
    grad_radial = grad_radial + jnp.dot(expansion, grad_pre, preferred_element_type=jnp.float32)
    return (grad_table, grad_radial, grad_filter)


def slot_mask(counts, slot_count):
    return (jnp.arange(slot_count, dtype=jnp.int32)[None, :] < counts[:, None]).astype(jnp.float32)


def atom_messages(indices, distances, counts, row_table, radial_weight, filter_weight):
    atom_count, slot_count = indices.shape
    block_rows = min(128, atom_count)
    pieces = (
        indices.reshape(-1, block_rows, slot_count),
        distances.reshape(-1, block_rows, slot_count),
        slot_mask(counts, slot_count).reshape(-1, block_rows, slot_count),
    )

    def one_block(portion):
        stored = edge_setup(
            portion[0], portion[1], portion[2], row_table, radial_weight, filter_weight
        )
        return edge_sums(stored, slot_count)

    return lax.map(one_block, pieces).reshape(atom_count, -1)


def atom_backward(
    indices, distances, counts, row_table, radial_weight, filter_weight, grad_message
):
    atom_count, slot_count = indices.shape
    block_rows = min(128, atom_count)
    pieces = (
        indices.reshape(-1, block_rows, slot_count),
        distances.reshape(-1, block_rows, slot_count),
        slot_mask(counts, slot_count).reshape(-1, block_rows, slot_count),
        grad_message.reshape(-1, block_rows, grad_message.shape[1]),
    )
    initial = (
        jnp.zeros(row_table.shape, jnp.float32),
        jnp.zeros(radial_weight.shape, jnp.float32),
        jnp.zeros(filter_weight.shape, jnp.float32),
    )

    def advance(totals, portion):
        stored = edge_setup(
            portion[0], portion[1], portion[2], row_table, radial_weight, filter_weight
        )
        return (edge_backward(stored, portion[0], filter_weight, portion[3], totals), None)

    return lax.scan(advance, initial, pieces)[0]


def probe_block(
    totals,
    indices,
    distances,
    cotangent,
    row_table,
    probe_radial,
    probe_filter,
    read_weight,
    final_weight,
):
    grad_table, grad_radial, grad_filter, grad_read, grad_final = totals
    stored = edge_setup(
        indices,
        distances,
        jnp.ones(indices.shape, jnp.float32),
        row_table,
        probe_radial,
        probe_filter,
    )
    packed = edge_sums(stored, indices.shape[1]).astype(jnp.bfloat16)
    read_pre = jnp.dot(packed, read_weight, preferred_element_type=jnp.float32)
    grad_final = grad_final + jnp.sum(cotangent[:, None] * shifted_plus(read_pre), axis=0)
    grad_inner = (cotangent[:, None] * final_weight[None, :] * jax.nn.sigmoid(read_pre)).astype(
        jnp.bfloat16
    )
    grad_read = grad_read + contract_rows(packed, grad_inner)
    grad_feats = contract_cols(grad_inner, read_weight)
    edge_totals = edge_backward(
        stored, indices, probe_filter, grad_feats, (grad_table, grad_radial, grad_filter)
    )
    return edge_totals + (grad_read, grad_final)


def interaction_head(atom_feats, kinds, species_gain, proj_input):
    onehot = (kinds[:, None] == jnp.arange(species_gain.shape[0], dtype=jnp.int32)[None, :]).astype(
        jnp.float32
    )
    gains = jnp.dot(onehot, species_gain, precision=lax.Precision.HIGHEST)
    scaled = (atom_feats.astype(jnp.float32) * gains).astype(jnp.bfloat16)
    projected = jnp.dot(scaled, proj_input, preferred_element_type=jnp.float32).astype(jnp.bfloat16)
    return (onehot, gains, scaled, projected)


def interaction_tail(atom_feats, message, mix_first, mix_second, proj_probe):
    packed_msg = message.astype(jnp.bfloat16)
    mix_pre = jnp.dot(packed_msg, mix_first, preferred_element_type=jnp.float32)
    activation = shifted_plus(mix_pre).astype(jnp.bfloat16)
    updated = (
        atom_feats.astype(jnp.float32)
        + jnp.dot(activation, mix_second, preferred_element_type=jnp.float32)
    ).astype(jnp.bfloat16)
    probe_proj = jnp.dot(updated, proj_probe, preferred_element_type=jnp.float32).astype(
        jnp.bfloat16
    )
    return (packed_msg, mix_pre, activation, updated, probe_proj)


def tail_backward(
    grad_proj, packed_msg, mix_pre, activation, updated, mix_first, mix_second, proj_probe
):
    grad_packed = grad_proj.astype(jnp.bfloat16)
    grad_proj_probe = contract_rows(updated, grad_packed)
    grad_updated = contract_cols(grad_packed, proj_probe)
    grad_upd_packed = grad_updated.astype(jnp.bfloat16)
    grad_mix_second = contract_rows(activation, grad_upd_packed)
    grad_mix_pre = (contract_cols(grad_upd_packed, mix_second) * jax.nn.sigmoid(mix_pre)).astype(
        jnp.bfloat16
    )
    grad_mix_first = contract_rows(packed_msg, grad_mix_pre)
    grad_message = contract_cols(grad_mix_pre, mix_first)
    return (grad_updated, grad_message, grad_proj_probe, grad_mix_second, grad_mix_first)


def head_backward(grad_proj, grad_updated, atom_feats, onehot, gains, scaled, proj_input):
    grad_packed = grad_proj.astype(jnp.bfloat16)
    grad_proj_input = contract_rows(scaled, grad_packed)
    grad_scaled = contract_cols(grad_packed, proj_input)
    d_features = grad_updated + grad_scaled * gains
    grad_gain = lax.dot_general(
        onehot,
        grad_scaled * atom_feats.astype(jnp.float32),
        (((0,), (0,)), ((), ())),
        precision=lax.Precision.HIGHEST,
    )
    return (d_features, grad_proj_input, grad_gain)


def add_rows(base, send_rows, returned):
    return base.at[send_rows.reshape(-1)].add(returned.reshape(-1, returned.shape[-1]))


def grid_of(blocks):
    empty = jnp.zeros((1,) + blocks.shape[1:], blocks.dtype)
    return jnp.concatenate([blocks[:4], empty, blocks[4:]], axis=0).reshape(
        (3, 3) + blocks.shape[1:]
    )


def blocks_of(layout):
    flat_grid = layout.reshape((9,) + layout.shape[2:])
    return jnp.concatenate([flat_grid[:4], flat_grid[5:]], axis=0)


def ghost_rows(blocks):
    layout = grid_of(blocks)
    padded = with_halo(layout, (("gx", 0), ("gy", 1)), 1)
    arrived = padded[0::2, 0::2]
    return blocks_of(arrived)


def ghost_grads(blocks):
    layout = grid_of(blocks)
    padded = with_halo(layout.astype(jnp.bfloat16), (("gx", 0), ("gy", 1)), 1).astype(layout.dtype)
    arrived = padded[0::2, 0::2]
    return blocks_of(arrived)


def per_device(
    features,
    species,
    atom_nbr,
    atom_nbr_count,
    atom_dist,
    send_list,
    probe_nbr,
    probe_dist,
    probe_count,
    d_density,
    species_gain,
    proj_input,
    atom_radial,
    atom_filter,
    mix_first,
    mix_second,
    proj_probe,
    probe_radial,
    probe_filter,
    read_weight,
    final_weight,
):
    atom_feats = features[0, 0, 0]
    atom_count = atom_feats.shape[0]
    feature_width = atom_feats.shape[1]
    send_rows = send_list[0, 0, 0]
    tile_nbr = atom_nbr[0, 0, 0]
    tile_dist = atom_dist[0, 0, 0]
    tile_counts = atom_nbr_count[0, 0, 0]
    onehot, gains, scaled, projected = interaction_head(
        atom_feats, species[0, 0, 0], species_gain, proj_input
    )
    row_table = jnp.concatenate(
        [projected, ghost_rows(projected[send_rows]).reshape(-1, feature_width)], axis=0
    )
    message = atom_messages(tile_nbr, tile_dist, tile_counts, row_table, atom_radial, atom_filter)
    packed_msg, mix_pre, activation, updated, probe_proj = interaction_tail(
        atom_feats, message, mix_first, mix_second, proj_probe
    )
    probe_table = jnp.concatenate(
        [probe_proj, ghost_rows(probe_proj[send_rows]).reshape(-1, feature_width)], axis=0
    )
    probe_ids = probe_nbr[0, 0, 0]
    probe_far = probe_dist[0, 0, 0]
    cotangents = d_density[0, 0, 0]
    block_rows = min(128, probe_ids.shape[0])
    active = probe_count[0, 0, 0]
    positions = jnp.arange(probe_ids.shape[0], dtype=jnp.int32)
    masked = cotangents * (positions < active).astype(jnp.float32)
    pieces = (
        probe_ids.reshape(-1, block_rows, probe_ids.shape[1]),
        probe_far.reshape(-1, block_rows, probe_far.shape[1]),
        masked.reshape(-1, block_rows),
    )
    initial = (
        jnp.zeros(probe_table.shape, jnp.float32),
        jnp.zeros(probe_radial.shape, jnp.float32),
        jnp.zeros(probe_filter.shape, jnp.float32),
        jnp.zeros(read_weight.shape, jnp.float32),
        jnp.zeros(final_weight.shape, jnp.float32),
    )

    def probe_turn(totals, portion):
        return (
            probe_block(
                totals,
                portion[0],
                portion[1],
                portion[2],
                probe_table,
                probe_radial,
                probe_filter,
                read_weight,
                final_weight,
            ),
            None,
        )

    grad_ptable, grad_pradial, grad_pfilter, grad_read, grad_final = lax.scan(
        probe_turn, initial, pieces
    )[0]
    probe_sums = lax.psum(
        jnp.concatenate(
            [
                grad_pfilter.reshape(-1),
                grad_read.reshape(-1),
                grad_pradial.reshape(-1),
                grad_final.reshape(-1),
            ]
        ),
        ("rep", "gx", "gy"),
    )
    returned_probe = ghost_grads(
        grad_ptable[atom_count:].reshape(send_rows.shape + (feature_width,))
    )
    grad_q = add_rows(grad_ptable[:atom_count], send_rows, returned_probe)
    grad_updated, grad_message, grad_proj_probe, grad_mix_second, grad_mix_first = tail_backward(
        grad_q, packed_msg, mix_pre, activation, updated, mix_first, mix_second, proj_probe
    )
    tail_part = jnp.concatenate(
        [grad_mix_first.reshape(-1), grad_mix_second.reshape(-1), grad_proj_probe.reshape(-1)]
    )
    tail_sums = lax.psum(tail_part, ("rep", "gx", "gy"))
    grad_atable, grad_aradial, grad_afilter = atom_backward(
        tile_nbr, tile_dist, tile_counts, row_table, atom_radial, atom_filter, grad_message
    )
    grad_atable, probe_sums, tail_sums = lax.optimization_barrier(
        (grad_atable, probe_sums, tail_sums)
    )
    returned_atom = ghost_grads(
        grad_atable[atom_count:].reshape(send_rows.shape + (feature_width,))
    )
    grad_u = add_rows(grad_atable[:atom_count], send_rows, returned_atom)
    d_features, grad_proj_input, grad_gain = head_backward(
        grad_u, grad_updated, atom_feats, onehot, gains, scaled, proj_input
    )
    atom_part = jnp.concatenate(
        [
            grad_afilter.reshape(-1),
            grad_proj_input.reshape(-1),
            grad_aradial.reshape(-1),
            grad_gain.reshape(-1),
        ]
    )
    atom_sums = lax.psum(atom_part, ("rep", "gx", "gy"))
    square = feature_width * feature_width
    radial = probe_radial.shape[0] * feature_width
    grad_square = jnp.concatenate(
        [
            probe_sums[: 2 * square],
            atom_sums[:square],
            atom_sums[square : 2 * square],
            tail_sums,
        ]
    ).reshape(7, feature_width, feature_width)
    grad_radial = jnp.concatenate(
        [probe_sums[2 * square : 2 * square + radial], atom_sums[2 * square : 2 * square + radial]]
    ).reshape(2, -1, feature_width)
    grad_vector = jnp.concatenate(
        [probe_sums[2 * square + radial :], atom_sums[2 * square + radial :]]
    ).reshape(-1, feature_width)
    return (d_features[None, None, None], grad_square, grad_radial, grad_vector)


def solution(mesh):
    in_specs = (
        P("rep", "gx", "gy", None, None),
        P("rep", "gx", "gy", None),
        P("rep", "gx", "gy", None, None),
        P("rep", "gx", "gy", None),
        P("rep", "gx", "gy", None, None),
        P("rep", "gx", "gy", None, None),
        P("rep", "gx", "gy", None, None),
        P("rep", "gx", "gy", None, None),
        P("rep", "gx", "gy"),
        P("rep", "gx", "gy", None),
        P(),
        P(),
        P(),
        P(),
        P(),
        P(),
        P(),
        P(),
        P(),
        P(),
        P(),
    )
    out_specs = (P("rep", "gx", "gy", None, None), P(), P(), P())
    return jax.shard_map(
        per_device, mesh=mesh, in_specs=in_specs, out_specs=out_specs, check_vma=False
    )
```

```python
import math

import jax
import jax.numpy as jnp
from jax import lax
from jax.sharding import PartitionSpec as P

cutoff_radius = 4.0


def with_halo(block, sides, width):
    for axis, dim in sides:
        count = lax.axis_size(axis)
        forward = [(i, i + 1) for i in range(count - 1)]
        forward.append((count - 1, 0))
        backward = [(target, source) for source, target in forward]
        low = lax.ppermute(
            lax.slice_in_dim(block, block.shape[dim] - width, None, axis=dim), axis, forward
        )
        high = lax.ppermute(lax.slice_in_dim(block, 0, width, axis=dim), axis, backward)
        block = jnp.concatenate([low, block, high], axis=dim)
    return block


def summed_everywhere(values, axes):
    for axis in axes:
        count = lax.axis_size(axis)
        stride = 1
        while stride < count:
            pairs = [(index, index ^ stride) for index in range(count)]
            values = values + lax.ppermute(values, axis, pairs)
            stride *= 2
    return values


def shifted_plus(values):
    return jax.nn.softplus(values) - math.log(2.0)


def contract_rows(former, latter):
    return lax.dot_general(
        former, latter, (((0,), (0,)), ((), ())), preferred_element_type=jnp.float32
    )


def contract_cols(former, latter):
    return lax.dot_general(
        former, latter, (((1,), (1,)), ((), ())), preferred_element_type=jnp.float32
    )


def one_hot_rows(indices, row_count):
    flat = indices.reshape(-1)
    return (flat[:, None] == jnp.arange(row_count, dtype=jnp.int32)[None, :]).astype(jnp.bfloat16)


def scatter_rows(selector, values):
    high = values.astype(jnp.bfloat16)
    low = (values - high.astype(jnp.float32)).astype(jnp.bfloat16)
    both = contract_rows(selector, jnp.concatenate([high, low], axis=1))
    return both[:, : values.shape[1]] + both[:, values.shape[1] :]


def edge_setup(indices, distances, live_mask, row_table, radial_weight, filter_weight):
    flat_dist = distances.reshape(-1)
    spacing = cutoff_radius / (radial_weight.shape[0] - 1)
    centers = jnp.arange(radial_weight.shape[0], dtype=jnp.float32) * spacing
    scaled = (flat_dist[None, :] - centers[:, None]) / spacing
    expansion = jnp.exp(-scaled * scaled).astype(jnp.bfloat16)
    pre_act = contract_rows(expansion, radial_weight)
    hidden = shifted_plus(pre_act).astype(jnp.bfloat16)
    envelope = 0.5 * (jnp.cos(math.pi * flat_dist / cutoff_radius) + 1.0) * live_mask.reshape(-1)
    filters = jnp.dot(hidden, filter_weight, preferred_element_type=jnp.float32) * envelope[:, None]
    selector = one_hot_rows(indices, row_table.shape[0])
    gathered = jnp.dot(selector, row_table, preferred_element_type=jnp.float32)
    return (expansion, pre_act, hidden, envelope, filters, gathered, selector)


def edge_sums(stored, slot_count):
    filters = stored[4]
    gathered = stored[5]
    terms = (gathered * filters).reshape(-1, slot_count, filters.shape[1])
    return jnp.sum(terms, axis=1)


def edge_backward(stored, indices, filter_weight, grad_message, totals):
    expansion, pre_act, hidden, envelope, filters, gathered, selector = stored
    grad_table, grad_radial, grad_filter = totals
    feature_width = grad_message.shape[1]
    spread = jnp.broadcast_to(
        grad_message[:, None, :], (grad_message.shape[0], indices.shape[1], feature_width)
    ).reshape(-1, feature_width)
    grad_table = grad_table + scatter_rows(selector, spread * filters)
    grad_out = (spread * gathered * envelope[:, None]).astype(jnp.bfloat16)
    grad_filter = grad_filter + contract_rows(hidden, grad_out)
    grad_pre = (contract_cols(grad_out, filter_weight) * jax.nn.sigmoid(pre_act)).astype(
        jnp.bfloat16
    )
    grad_radial = grad_radial + jnp.dot(expansion, grad_pre, preferred_element_type=jnp.float32)
    return (grad_table, grad_radial, grad_filter)


def slot_mask(counts, slot_count):
    return (jnp.arange(slot_count, dtype=jnp.int32)[None, :] < counts[:, None]).astype(jnp.float32)


def atom_messages(indices, distances, counts, row_table, radial_weight, filter_weight):
    atom_count, slot_count = indices.shape
    block_rows = min(128, atom_count)
    pieces = (
        indices.reshape(-1, block_rows, slot_count),
        distances.reshape(-1, block_rows, slot_count),
        slot_mask(counts, slot_count).reshape(-1, block_rows, slot_count),
    )

    def one_block(portion):
        stored = edge_setup(
            portion[0], portion[1], portion[2], row_table, radial_weight, filter_weight
        )
        return edge_sums(stored, slot_count)

    return lax.map(one_block, pieces).reshape(atom_count, -1)


def atom_backward(
    indices, distances, counts, row_table, radial_weight, filter_weight, grad_message
):
    atom_count, slot_count = indices.shape
    block_rows = min(128, atom_count)
    pieces = (
        indices.reshape(-1, block_rows, slot_count),
        distances.reshape(-1, block_rows, slot_count),
        slot_mask(counts, slot_count).reshape(-1, block_rows, slot_count),
        grad_message.reshape(-1, block_rows, grad_message.shape[1]),
    )
    initial = (
        jnp.zeros(row_table.shape, jnp.float32),
        jnp.zeros(radial_weight.shape, jnp.float32),
        jnp.zeros(filter_weight.shape, jnp.float32),
    )

    def advance(totals, portion):
        stored = edge_setup(
            portion[0], portion[1], portion[2], row_table, radial_weight, filter_weight
        )
        return (edge_backward(stored, portion[0], filter_weight, portion[3], totals), None)

    return lax.scan(advance, initial, pieces)[0]


def probe_block(
    totals,
    indices,
    distances,
    cotangent,
    row_table,
    probe_radial,
    probe_filter,
    read_weight,
    final_weight,
):
    grad_table, grad_radial, grad_filter, grad_read, grad_final = totals
    stored = edge_setup(
        indices,
        distances,
        jnp.ones(indices.shape, jnp.float32),
        row_table,
        probe_radial,
        probe_filter,
    )
    packed = edge_sums(stored, indices.shape[1]).astype(jnp.bfloat16)
    read_pre = jnp.dot(packed, read_weight, preferred_element_type=jnp.float32)
    grad_final = grad_final + jnp.sum(cotangent[:, None] * shifted_plus(read_pre), axis=0)
    grad_inner = (cotangent[:, None] * final_weight[None, :] * jax.nn.sigmoid(read_pre)).astype(
        jnp.bfloat16
    )
    grad_read = grad_read + contract_rows(packed, grad_inner)
    grad_feats = contract_cols(grad_inner, read_weight)
    edge_totals = edge_backward(
        stored, indices, probe_filter, grad_feats, (grad_table, grad_radial, grad_filter)
    )
    return edge_totals + (grad_read, grad_final)


def interaction_head(atom_feats, kinds, species_gain, proj_input):
    onehot = (kinds[:, None] == jnp.arange(species_gain.shape[0], dtype=jnp.int32)[None, :]).astype(
        jnp.float32
    )
    gains = jnp.dot(onehot, species_gain, precision=lax.Precision.HIGHEST)
    scaled = (atom_feats.astype(jnp.float32) * gains).astype(jnp.bfloat16)
    projected = jnp.dot(scaled, proj_input, preferred_element_type=jnp.float32).astype(jnp.bfloat16)
    return (onehot, gains, scaled, projected)


def interaction_tail(atom_feats, message, mix_first, mix_second, proj_probe):
    packed_msg = message.astype(jnp.bfloat16)
    mix_pre = jnp.dot(packed_msg, mix_first, preferred_element_type=jnp.float32)
    activation = shifted_plus(mix_pre).astype(jnp.bfloat16)
    updated = (
        atom_feats.astype(jnp.float32)
        + jnp.dot(activation, mix_second, preferred_element_type=jnp.float32)
    ).astype(jnp.bfloat16)
    probe_proj = jnp.dot(updated, proj_probe, preferred_element_type=jnp.float32).astype(
        jnp.bfloat16
    )
    return (packed_msg, mix_pre, activation, updated, probe_proj)


def tail_backward(
    grad_proj, packed_msg, mix_pre, activation, updated, mix_first, mix_second, proj_probe
):
    grad_packed = grad_proj.astype(jnp.bfloat16)
    grad_proj_probe = contract_rows(updated, grad_packed)
    grad_updated = contract_cols(grad_packed, proj_probe)
    grad_upd_packed = grad_updated.astype(jnp.bfloat16)
    grad_mix_second = contract_rows(activation, grad_upd_packed)
    grad_mix_pre = (contract_cols(grad_upd_packed, mix_second) * jax.nn.sigmoid(mix_pre)).astype(
        jnp.bfloat16
    )
    grad_mix_first = contract_rows(packed_msg, grad_mix_pre)
    grad_message = contract_cols(grad_mix_pre, mix_first)
    return (grad_updated, grad_message, grad_proj_probe, grad_mix_second, grad_mix_first)


def head_backward(grad_proj, grad_updated, atom_feats, onehot, gains, scaled, proj_input):
    grad_packed = grad_proj.astype(jnp.bfloat16)
    grad_proj_input = contract_rows(scaled, grad_packed)
    grad_scaled = contract_cols(grad_packed, proj_input)
    d_features = grad_updated + grad_scaled * gains
    grad_gain = lax.dot_general(
        onehot,
        grad_scaled * atom_feats.astype(jnp.float32),
        (((0,), (0,)), ((), ())),
        precision=lax.Precision.HIGHEST,
    )
    return (d_features, grad_proj_input, grad_gain)


def add_rows(base, send_rows, returned):
    return base.at[send_rows.reshape(-1)].add(returned.reshape(-1, returned.shape[-1]))


def grid_of(blocks):
    empty = jnp.zeros((1,) + blocks.shape[1:], blocks.dtype)
    return jnp.concatenate([blocks[:4], empty, blocks[4:]], axis=0).reshape(
        (3, 3) + blocks.shape[1:]
    )


def blocks_of(layout):
    flat_grid = layout.reshape((9,) + layout.shape[2:])
    return jnp.concatenate([flat_grid[:4], flat_grid[5:]], axis=0)


def ghost_rows(blocks):
    layout = grid_of(blocks)
    padded = with_halo(layout, (("gx", 0), ("gy", 1)), 1)
    arrived = padded[0::2, 0::2]
    return blocks_of(arrived)


def ghost_grads(blocks):
    layout = grid_of(blocks)
    padded = with_halo(layout.astype(jnp.bfloat16), (("gx", 0), ("gy", 1)), 1).astype(layout.dtype)
    arrived = padded[0::2, 0::2]
    return blocks_of(arrived)


def per_device(
    features,
    species,
    atom_nbr,
    atom_nbr_count,
    atom_dist,
    send_list,
    probe_nbr,
    probe_dist,
    probe_count,
    d_density,
    species_gain,
    proj_input,
    atom_radial,
    atom_filter,
    mix_first,
    mix_second,
    proj_probe,
    probe_radial,
    probe_filter,
    read_weight,
    final_weight,
):
    atom_feats = features[0, 0, 0]
    atom_count = atom_feats.shape[0]
    feature_width = atom_feats.shape[1]
    send_rows = send_list[0, 0, 0]
    tile_nbr = atom_nbr[0, 0, 0]
    tile_dist = atom_dist[0, 0, 0]
    tile_counts = atom_nbr_count[0, 0, 0]
    onehot, gains, scaled, projected = interaction_head(
        atom_feats, species[0, 0, 0], species_gain, proj_input
    )
    row_table = jnp.concatenate(
        [projected, ghost_rows(projected[send_rows]).reshape(-1, feature_width)], axis=0
    )
    message = atom_messages(tile_nbr, tile_dist, tile_counts, row_table, atom_radial, atom_filter)
    packed_msg, mix_pre, activation, updated, probe_proj = interaction_tail(
        atom_feats, message, mix_first, mix_second, proj_probe
    )
    probe_table = jnp.concatenate(
        [probe_proj, ghost_rows(probe_proj[send_rows]).reshape(-1, feature_width)], axis=0
    )
    probe_ids = probe_nbr[0, 0, 0]
    probe_far = probe_dist[0, 0, 0]
    cotangents = d_density[0, 0, 0]
    block_rows = min(128, probe_ids.shape[0])
    active = probe_count[0, 0, 0]
    positions = jnp.arange(probe_ids.shape[0], dtype=jnp.int32)
    masked = cotangents * (positions < active).astype(jnp.float32)
    pieces = (
        probe_ids.reshape(-1, block_rows, probe_ids.shape[1]),
        probe_far.reshape(-1, block_rows, probe_far.shape[1]),
        masked.reshape(-1, block_rows),
    )
    initial = (
        jnp.zeros(probe_table.shape, jnp.float32),
        jnp.zeros(probe_radial.shape, jnp.float32),
        jnp.zeros(probe_filter.shape, jnp.float32),
        jnp.zeros(read_weight.shape, jnp.float32),
        jnp.zeros(final_weight.shape, jnp.float32),
    )

    def probe_turn(totals, portion):
        return (
            probe_block(
                totals,
                portion[0],
                portion[1],
                portion[2],
                probe_table,
                probe_radial,
                probe_filter,
                read_weight,
                final_weight,
            ),
            None,
        )

    grad_ptable, grad_pradial, grad_pfilter, grad_read, grad_final = lax.scan(
        probe_turn, initial, pieces
    )[0]
    probe_part = jnp.concatenate(
        [
            grad_pfilter.reshape(-1),
            grad_read.reshape(-1),
            grad_pradial.reshape(-1),
            grad_final.reshape(-1),
        ]
    )
    returned_probe = ghost_grads(
        grad_ptable[atom_count:].reshape(send_rows.shape + (feature_width,))
    )
    grad_q = add_rows(grad_ptable[:atom_count], send_rows, returned_probe)
    grad_updated, grad_message, grad_proj_probe, grad_mix_second, grad_mix_first = tail_backward(
        grad_q, packed_msg, mix_pre, activation, updated, mix_first, mix_second, proj_probe
    )
    tail_part = jnp.concatenate(
        [grad_mix_first.reshape(-1), grad_mix_second.reshape(-1), grad_proj_probe.reshape(-1)]
    )
    grad_atable, grad_aradial, grad_afilter = atom_backward(
        tile_nbr, tile_dist, tile_counts, row_table, atom_radial, atom_filter, grad_message
    )
    returned_atom = ghost_grads(
        grad_atable[atom_count:].reshape(send_rows.shape + (feature_width,))
    )
    grad_u = add_rows(grad_atable[:atom_count], send_rows, returned_atom)
    d_features, grad_proj_input, grad_gain = head_backward(
        grad_u, grad_updated, atom_feats, onehot, gains, scaled, proj_input
    )
    atom_part = jnp.concatenate(
        [
            grad_afilter.reshape(-1),
            grad_proj_input.reshape(-1),
            grad_aradial.reshape(-1),
            grad_gain.reshape(-1),
        ]
    )
    sums = summed_everywhere(
        jnp.concatenate([probe_part, tail_part, atom_part]), ("gy", "gx", "rep")
    )
    probe_sums = sums[: probe_part.shape[0]]
    tail_sums = sums[probe_part.shape[0] : probe_part.shape[0] + tail_part.shape[0]]
    atom_sums = sums[probe_part.shape[0] + tail_part.shape[0] :]
    square = feature_width * feature_width
    radial = probe_radial.shape[0] * feature_width
    grad_square = jnp.concatenate(
        [
            probe_sums[: 2 * square],
            atom_sums[:square],
            atom_sums[square : 2 * square],
            tail_sums,
        ]
    ).reshape(7, feature_width, feature_width)
    grad_radial = jnp.concatenate(
        [probe_sums[2 * square : 2 * square + radial], atom_sums[2 * square : 2 * square + radial]]
    ).reshape(2, -1, feature_width)
    grad_vector = jnp.concatenate(
        [probe_sums[2 * square + radial :], atom_sums[2 * square + radial :]]
    ).reshape(-1, feature_width)
    return (d_features[None, None, None], grad_square, grad_radial, grad_vector)


def solution(mesh):
    in_specs = (
        P("rep", "gx", "gy", None, None),
        P("rep", "gx", "gy", None),
        P("rep", "gx", "gy", None, None),
        P("rep", "gx", "gy", None),
        P("rep", "gx", "gy", None, None),
        P("rep", "gx", "gy", None, None),
        P("rep", "gx", "gy", None, None),
        P("rep", "gx", "gy", None, None),
        P("rep", "gx", "gy"),
        P("rep", "gx", "gy", None),
        P(),
        P(),
        P(),
        P(),
        P(),
        P(),
        P(),
        P(),
        P(),
        P(),
        P(),
    )
    out_specs = (P("rep", "gx", "gy", None, None), P(), P(), P())
    return jax.shard_map(
        per_device, mesh=mesh, in_specs=in_specs, out_specs=out_specs, check_vma=False
    )
```

```python
import math

import jax
import jax.numpy as jnp
from jax import lax
from jax.sharding import PartitionSpec as P

cutoff_radius = 4.0


def with_halo(block, sides, width):
    for axis, dim in sides:
        count = lax.axis_size(axis)
        forward = [(i, i + 1) for i in range(count - 1)]
        forward.append((count - 1, 0))
        backward = [(target, source) for source, target in forward]
        low = lax.ppermute(
            lax.slice_in_dim(block, block.shape[dim] - width, None, axis=dim), axis, forward
        )
        high = lax.ppermute(lax.slice_in_dim(block, 0, width, axis=dim), axis, backward)
        block = jnp.concatenate([low, block, high], axis=dim)
    return block


def doubling_steps(axes):
    steps = []
    for axis in axes:
        stride = 1
        while stride < lax.axis_size(axis):
            steps.append((axis, stride))
            stride *= 2
    return steps


def doubling_step(values, step):
    axis, stride = step
    pairs = [(index, index ^ stride) for index in range(lax.axis_size(axis))]
    return values + lax.ppermute(values, axis, pairs)


def summed_everywhere(values, axes):
    for axis in axes:
        count = lax.axis_size(axis)
        stride = 1
        while stride < count:
            pairs = [(index, index ^ stride) for index in range(count)]
            values = values + lax.ppermute(values, axis, pairs)
            stride *= 2
    return values


def shifted_plus(values):
    return jax.nn.softplus(values) - math.log(2.0)


def contract_rows(former, latter):
    return lax.dot_general(
        former, latter, (((0,), (0,)), ((), ())), preferred_element_type=jnp.float32
    )


def contract_cols(former, latter):
    return lax.dot_general(
        former, latter, (((1,), (1,)), ((), ())), preferred_element_type=jnp.float32
    )


def one_hot_rows(indices, row_count):
    flat = indices.reshape(-1)
    return (flat[:, None] == jnp.arange(row_count, dtype=jnp.int32)[None, :]).astype(jnp.bfloat16)


def scatter_rows(selector, values):
    return contract_rows(selector, values.astype(jnp.bfloat16))


def edge_setup(indices, distances, live_mask, row_table, radial_weight, filter_weight):
    flat_dist = distances.reshape(-1)
    spacing = cutoff_radius / (radial_weight.shape[0] - 1)
    centers = jnp.arange(radial_weight.shape[0], dtype=jnp.float32) * spacing
    scaled = (flat_dist[None, :] - centers[:, None]) / spacing
    expansion = jnp.exp(-scaled * scaled).astype(jnp.bfloat16)
    pre_act = contract_rows(expansion, radial_weight)
    hidden = shifted_plus(pre_act).astype(jnp.bfloat16)
    envelope = 0.5 * (jnp.cos(math.pi * flat_dist / cutoff_radius) + 1.0) * live_mask.reshape(-1)
    filters = jnp.dot(hidden, filter_weight, preferred_element_type=jnp.float32) * envelope[:, None]
    selector = one_hot_rows(indices, row_table.shape[0])
    gathered = jnp.dot(selector, row_table, preferred_element_type=jnp.float32)
    return (expansion, pre_act, hidden, envelope, filters, gathered, selector)


def edge_sums(stored, slot_count):
    filters = stored[4]
    gathered = stored[5]
    terms = (gathered * filters).reshape(-1, slot_count, filters.shape[1])
    return jnp.sum(terms, axis=1)


def edge_backward(stored, indices, filter_weight, grad_message, totals):
    expansion, pre_act, hidden, envelope, filters, gathered, selector = stored
    grad_table, grad_radial, grad_filter = totals
    feature_width = grad_message.shape[1]
    spread = jnp.broadcast_to(
        grad_message[:, None, :], (grad_message.shape[0], indices.shape[1], feature_width)
    ).reshape(-1, feature_width)
    grad_table = grad_table + scatter_rows(selector, spread * filters)
    grad_out = (spread * gathered * envelope[:, None]).astype(jnp.bfloat16)
    grad_filter = grad_filter + contract_rows(hidden, grad_out)
    grad_pre = (contract_cols(grad_out, filter_weight) * jax.nn.sigmoid(pre_act)).astype(
        jnp.bfloat16
    )
    grad_radial = grad_radial + jnp.dot(expansion, grad_pre, preferred_element_type=jnp.float32)
    return (grad_table, grad_radial, grad_filter)


def slot_mask(counts, slot_count):
    return (jnp.arange(slot_count, dtype=jnp.int32)[None, :] < counts[:, None]).astype(jnp.float32)


def atom_messages(indices, distances, counts, row_table, radial_weight, filter_weight):
    atom_count, slot_count = indices.shape
    block_rows = min(128, atom_count)
    pieces = (
        indices.reshape(-1, block_rows, slot_count),
        distances.reshape(-1, block_rows, slot_count),
        slot_mask(counts, slot_count).reshape(-1, block_rows, slot_count),
    )

    def one_block(portion):
        stored = edge_setup(
            portion[0], portion[1], portion[2], row_table, radial_weight, filter_weight
        )
        return edge_sums(stored, slot_count)

    return lax.map(one_block, pieces).reshape(atom_count, -1)


def atom_backward(
    indices, distances, counts, row_table, radial_weight, filter_weight, grad_message, early
):
    atom_count, slot_count = indices.shape
    block_rows = min(128, atom_count)
    pieces = (
        indices.reshape(-1, block_rows, slot_count),
        distances.reshape(-1, block_rows, slot_count),
        slot_mask(counts, slot_count).reshape(-1, block_rows, slot_count),
        grad_message.reshape(-1, block_rows, grad_message.shape[1]),
    )
    initial = (
        jnp.zeros(row_table.shape, jnp.float32),
        jnp.zeros(radial_weight.shape, jnp.float32),
        jnp.zeros(filter_weight.shape, jnp.float32),
    )

    steps = doubling_steps(("gy", "gx", "rep"))
    block_count = pieces[0].shape[0]
    per_block = -(-len(steps) // block_count)
    totals = initial
    for block in range(block_count):
        portion = tuple(piece[block] for piece in pieces)
        stored = edge_setup(
            portion[0], portion[1], portion[2], row_table, radial_weight, filter_weight
        )
        totals = edge_backward(stored, portion[0], filter_weight, portion[3], totals)
        for step in steps[block * per_block : (block + 1) * per_block]:
            early = doubling_step(early, step)
        totals, early = lax.optimization_barrier((totals, early))
    return totals, early


def probe_block(
    totals,
    indices,
    distances,
    cotangent,
    row_table,
    probe_radial,
    probe_filter,
    read_weight,
    final_weight,
):
    grad_table, grad_radial, grad_filter, grad_read, grad_final = totals
    stored = edge_setup(
        indices,
        distances,
        jnp.ones(indices.shape, jnp.float32),
        row_table,
        probe_radial,
        probe_filter,
    )
    packed = edge_sums(stored, indices.shape[1]).astype(jnp.bfloat16)
    read_pre = jnp.dot(packed, read_weight, preferred_element_type=jnp.float32)
    grad_final = grad_final + jnp.sum(cotangent[:, None] * shifted_plus(read_pre), axis=0)
    grad_inner = (cotangent[:, None] * final_weight[None, :] * jax.nn.sigmoid(read_pre)).astype(
        jnp.bfloat16
    )
    grad_read = grad_read + contract_rows(packed, grad_inner)
    grad_feats = contract_cols(grad_inner, read_weight)
    edge_totals = edge_backward(
        stored, indices, probe_filter, grad_feats, (grad_table, grad_radial, grad_filter)
    )
    return edge_totals + (grad_read, grad_final)


def interaction_head(atom_feats, kinds, species_gain, proj_input):
    onehot = (kinds[:, None] == jnp.arange(species_gain.shape[0], dtype=jnp.int32)[None, :]).astype(
        jnp.float32
    )
    gains = jnp.dot(onehot, species_gain, precision=lax.Precision.HIGHEST)
    scaled = (atom_feats.astype(jnp.float32) * gains).astype(jnp.bfloat16)
    projected = jnp.dot(scaled, proj_input, preferred_element_type=jnp.float32).astype(jnp.bfloat16)
    return (onehot, gains, scaled, projected)


def interaction_tail(atom_feats, message, mix_first, mix_second, proj_probe):
    packed_msg = message.astype(jnp.bfloat16)
    mix_pre = jnp.dot(packed_msg, mix_first, preferred_element_type=jnp.float32)
    activation = shifted_plus(mix_pre).astype(jnp.bfloat16)
    updated = (
        atom_feats.astype(jnp.float32)
        + jnp.dot(activation, mix_second, preferred_element_type=jnp.float32)
    ).astype(jnp.bfloat16)
    probe_proj = jnp.dot(updated, proj_probe, preferred_element_type=jnp.float32).astype(
        jnp.bfloat16
    )
    return (packed_msg, mix_pre, activation, updated, probe_proj)


def tail_backward(
    grad_proj, packed_msg, mix_pre, activation, updated, mix_first, mix_second, proj_probe
):
    grad_packed = grad_proj.astype(jnp.bfloat16)
    grad_proj_probe = contract_rows(updated, grad_packed)
    grad_updated = contract_cols(grad_packed, proj_probe)
    grad_upd_packed = grad_updated.astype(jnp.bfloat16)
    grad_mix_second = contract_rows(activation, grad_upd_packed)
    grad_mix_pre = (contract_cols(grad_upd_packed, mix_second) * jax.nn.sigmoid(mix_pre)).astype(
        jnp.bfloat16
    )
    grad_mix_first = contract_rows(packed_msg, grad_mix_pre)
    grad_message = contract_cols(grad_mix_pre, mix_first)
    return (grad_updated, grad_message, grad_proj_probe, grad_mix_second, grad_mix_first)


def head_backward(grad_proj, grad_updated, atom_feats, onehot, gains, scaled, proj_input):
    grad_packed = grad_proj.astype(jnp.bfloat16)
    grad_proj_input = contract_rows(scaled, grad_packed)
    grad_scaled = contract_cols(grad_packed, proj_input)
    d_features = grad_updated + grad_scaled * gains
    grad_gain = lax.dot_general(
        onehot,
        grad_scaled * atom_feats.astype(jnp.float32),
        (((0,), (0,)), ((), ())),
        precision=lax.Precision.HIGHEST,
    )
    return (d_features, grad_proj_input, grad_gain)


def add_rows(base, send_rows, returned):
    return base.at[send_rows.reshape(-1)].add(returned.reshape(-1, returned.shape[-1]))


def grid_of(blocks):
    empty = jnp.zeros((1,) + blocks.shape[1:], blocks.dtype)
    return jnp.concatenate([blocks[:4], empty, blocks[4:]], axis=0).reshape(
        (3, 3) + blocks.shape[1:]
    )


def blocks_of(layout):
    flat_grid = layout.reshape((9,) + layout.shape[2:])
    return jnp.concatenate([flat_grid[:4], flat_grid[5:]], axis=0)


def ghost_rows(blocks):
    layout = grid_of(blocks)
    padded = with_halo(layout, (("gx", 0), ("gy", 1)), 1)
    arrived = padded[0::2, 0::2]
    return blocks_of(arrived)


def ghost_grads(blocks):
    layout = grid_of(blocks)
    padded = with_halo(layout.astype(jnp.bfloat16), (("gx", 0), ("gy", 1)), 1).astype(layout.dtype)
    arrived = padded[0::2, 0::2]
    return blocks_of(arrived)


def per_device(
    features,
    species,
    atom_nbr,
    atom_nbr_count,
    atom_dist,
    send_list,
    probe_nbr,
    probe_dist,
    probe_count,
    d_density,
    species_gain,
    proj_input,
    atom_radial,
    atom_filter,
    mix_first,
    mix_second,
    proj_probe,
    probe_radial,
    probe_filter,
    read_weight,
    final_weight,
):
    atom_feats = features[0, 0, 0]
    atom_count = atom_feats.shape[0]
    feature_width = atom_feats.shape[1]
    send_rows = send_list[0, 0, 0]
    tile_nbr = atom_nbr[0, 0, 0]
    tile_dist = atom_dist[0, 0, 0]
    tile_counts = atom_nbr_count[0, 0, 0]
    onehot, gains, scaled, projected = interaction_head(
        atom_feats, species[0, 0, 0], species_gain, proj_input
    )
    row_table = jnp.concatenate(
        [projected, ghost_rows(projected[send_rows]).reshape(-1, feature_width)], axis=0
    )
    message = atom_messages(tile_nbr, tile_dist, tile_counts, row_table, atom_radial, atom_filter)
    packed_msg, mix_pre, activation, updated, probe_proj = interaction_tail(
        atom_feats, message, mix_first, mix_second, proj_probe
    )
    probe_table = jnp.concatenate(
        [probe_proj, ghost_rows(probe_proj[send_rows]).reshape(-1, feature_width)], axis=0
    )
    probe_ids = probe_nbr[0, 0, 0]
    probe_far = probe_dist[0, 0, 0]
    cotangents = d_density[0, 0, 0]
    block_rows = min(128, probe_ids.shape[0])
    active = probe_count[0, 0, 0]
    positions = jnp.arange(probe_ids.shape[0], dtype=jnp.int32)
    masked = cotangents * (positions < active).astype(jnp.float32)
    pieces = (
        probe_ids.reshape(-1, block_rows, probe_ids.shape[1]),
        probe_far.reshape(-1, block_rows, probe_far.shape[1]),
        masked.reshape(-1, block_rows),
    )
    initial = (
        jnp.zeros(probe_table.shape, jnp.float32),
        jnp.zeros(probe_radial.shape, jnp.float32),
        jnp.zeros(probe_filter.shape, jnp.float32),
        jnp.zeros(read_weight.shape, jnp.float32),
        jnp.zeros(final_weight.shape, jnp.float32),
    )

    def probe_turn(totals, portion):
        return (
            probe_block(
                totals,
                portion[0],
                portion[1],
                portion[2],
                probe_table,
                probe_radial,
                probe_filter,
                read_weight,
                final_weight,
            ),
            None,
        )

    grad_ptable, grad_pradial, grad_pfilter, grad_read, grad_final = lax.scan(
        probe_turn, initial, pieces
    )[0]
    probe_part = jnp.concatenate(
        [
            grad_pfilter.reshape(-1),
            grad_read.reshape(-1),
            grad_pradial.reshape(-1),
            grad_final.reshape(-1),
        ]
    )
    returned_probe = ghost_grads(
        grad_ptable[atom_count:].reshape(send_rows.shape + (feature_width,))
    )
    grad_q = add_rows(grad_ptable[:atom_count], send_rows, returned_probe)
    grad_updated, grad_message, grad_proj_probe, grad_mix_second, grad_mix_first = tail_backward(
        grad_q, packed_msg, mix_pre, activation, updated, mix_first, mix_second, proj_probe
    )
    tail_part = jnp.concatenate(
        [grad_mix_first.reshape(-1), grad_mix_second.reshape(-1), grad_proj_probe.reshape(-1)]
    )
    (grad_atable, grad_aradial, grad_afilter), early_sums = atom_backward(
        tile_nbr,
        tile_dist,
        tile_counts,
        row_table,
        atom_radial,
        atom_filter,
        grad_message,
        jnp.concatenate([probe_part, tail_part]),
    )
    returned_atom = ghost_grads(
        grad_atable[atom_count:].reshape(send_rows.shape + (feature_width,))
    )
    grad_u = add_rows(grad_atable[:atom_count], send_rows, returned_atom)
    d_features, grad_proj_input, grad_gain = head_backward(
        grad_u, grad_updated, atom_feats, onehot, gains, scaled, proj_input
    )
    atom_part = jnp.concatenate(
        [
            grad_afilter.reshape(-1),
            grad_proj_input.reshape(-1),
            grad_aradial.reshape(-1),
            grad_gain.reshape(-1),
        ]
    )
    atom_sums = summed_everywhere(atom_part, ("gy", "gx", "rep"))
    probe_sums = early_sums[: probe_part.shape[0]]
    tail_sums = early_sums[probe_part.shape[0] :]
    square = feature_width * feature_width
    radial = probe_radial.shape[0] * feature_width
    grad_square = jnp.concatenate(
        [
            probe_sums[: 2 * square],
            atom_sums[:square],
            atom_sums[square : 2 * square],
            tail_sums,
        ]
    ).reshape(7, feature_width, feature_width)
    grad_radial = jnp.concatenate(
        [probe_sums[2 * square : 2 * square + radial], atom_sums[2 * square : 2 * square + radial]]
    ).reshape(2, -1, feature_width)
    grad_vector = jnp.concatenate(
        [probe_sums[2 * square + radial :], atom_sums[2 * square + radial :]]
    ).reshape(-1, feature_width)
    return (d_features[None, None, None], grad_square, grad_radial, grad_vector)


def solution(mesh):
    in_specs = (
        P("rep", "gx", "gy", None, None),
        P("rep", "gx", "gy", None),
        P("rep", "gx", "gy", None, None),
        P("rep", "gx", "gy", None),
        P("rep", "gx", "gy", None, None),
        P("rep", "gx", "gy", None, None),
        P("rep", "gx", "gy", None, None),
        P("rep", "gx", "gy", None, None),
        P("rep", "gx", "gy"),
        P("rep", "gx", "gy", None),
        P(),
        P(),
        P(),
        P(),
        P(),
        P(),
        P(),
        P(),
        P(),
        P(),
        P(),
    )
    out_specs = (P("rep", "gx", "gy", None, None), P(), P(), P())
    return jax.shard_map(
        per_device, mesh=mesh, in_specs=in_specs, out_specs=out_specs, check_vma=False
    )
```

```python
import math

import jax
import jax.numpy as jnp
from jax import lax
from jax.sharding import PartitionSpec as P

cutoff_radius = 4.0


def with_halo(block, sides, width):
    for axis, dim in sides:
        count = lax.axis_size(axis)
        forward = [(i, i + 1) for i in range(count - 1)]
        forward.append((count - 1, 0))
        backward = [(target, source) for source, target in forward]
        low = lax.ppermute(
            lax.slice_in_dim(block, block.shape[dim] - width, None, axis=dim), axis, forward
        )
        high = lax.ppermute(lax.slice_in_dim(block, 0, width, axis=dim), axis, backward)
        block = jnp.concatenate([low, block, high], axis=dim)
    return block


def doubling_steps(axes):
    steps = []
    for axis in axes:
        stride = 1
        while stride < lax.axis_size(axis):
            steps.append((axis, stride))
            stride *= 2
    return steps


def doubling_step(values, step):
    axis, stride = step
    pairs = [(index, index ^ stride) for index in range(lax.axis_size(axis))]
    return values + lax.ppermute(values, axis, pairs)


def summed_everywhere(values, axes):
    for axis in axes:
        count = lax.axis_size(axis)
        stride = 1
        while stride < count:
            pairs = [(index, index ^ stride) for index in range(count)]
            values = values + lax.ppermute(values, axis, pairs)
            stride *= 2
    return values


def shifted_plus(values):
    return jax.nn.softplus(values) - math.log(2.0)


def contract_rows(former, latter):
    return lax.dot_general(
        former, latter, (((0,), (0,)), ((), ())), preferred_element_type=jnp.float32
    )


def contract_cols(former, latter):
    return lax.dot_general(
        former, latter, (((1,), (1,)), ((), ())), preferred_element_type=jnp.float32
    )


def one_hot_rows(indices, row_count):
    flat = indices.reshape(-1)
    return (flat[:, None] == jnp.arange(row_count, dtype=jnp.int32)[None, :]).astype(jnp.bfloat16)


def scatter_rows(indices, row_count, values):
    flat = indices.reshape(-1)
    spread = (jnp.arange(row_count, dtype=jnp.int32)[:, None] == flat[None, :]).astype(jnp.bfloat16)
    return jnp.dot(spread, values.astype(jnp.bfloat16), preferred_element_type=jnp.float32)


def edge_setup(indices, distances, live_mask, row_table, radial_weight, filter_weight):
    flat_dist = distances.reshape(-1)
    spacing = cutoff_radius / (radial_weight.shape[0] - 1)
    centers = jnp.arange(radial_weight.shape[0], dtype=jnp.float32) * spacing
    scaled = (flat_dist[None, :] - centers[:, None]) / spacing
    expansion = jnp.exp(-scaled * scaled).astype(jnp.bfloat16)
    pre_act = contract_rows(expansion, radial_weight)
    hidden = shifted_plus(pre_act).astype(jnp.bfloat16)
    envelope = 0.5 * (jnp.cos(math.pi * flat_dist / cutoff_radius) + 1.0) * live_mask.reshape(-1)
    filters = jnp.dot(hidden, filter_weight, preferred_element_type=jnp.float32) * envelope[:, None]
    selector = one_hot_rows(indices, row_table.shape[0])
    gathered = jnp.dot(selector, row_table, preferred_element_type=jnp.float32)
    return (expansion, pre_act, hidden, envelope, filters, gathered, selector)


def edge_sums(stored, slot_count):
    filters = stored[4]
    gathered = stored[5]
    terms = (gathered * filters).reshape(-1, slot_count, filters.shape[1])
    return jnp.sum(terms, axis=1)


def edge_backward(stored, indices, filter_weight, grad_message, totals):
    expansion, pre_act, hidden, envelope, filters, gathered, selector = stored
    grad_table, grad_radial, grad_filter = totals
    feature_width = grad_message.shape[1]
    spread = jnp.broadcast_to(
        grad_message[:, None, :], (grad_message.shape[0], indices.shape[1], feature_width)
    ).reshape(-1, feature_width)
    grad_table = grad_table + scatter_rows(indices, grad_table.shape[0], spread * filters)
    grad_out = (spread * gathered * envelope[:, None]).astype(jnp.bfloat16)
    grad_filter = grad_filter + contract_rows(hidden, grad_out)
    grad_pre = (contract_cols(grad_out, filter_weight) * jax.nn.sigmoid(pre_act)).astype(
        jnp.bfloat16
    )
    grad_radial = grad_radial + jnp.dot(expansion, grad_pre, preferred_element_type=jnp.float32)
    return (grad_table, grad_radial, grad_filter)


def slot_mask(counts, slot_count):
    return (jnp.arange(slot_count, dtype=jnp.int32)[None, :] < counts[:, None]).astype(jnp.float32)


def atom_messages(indices, distances, counts, row_table, radial_weight, filter_weight):
    atom_count, slot_count = indices.shape
    block_rows = min(128, atom_count)
    pieces = (
        indices.reshape(-1, block_rows, slot_count),
        distances.reshape(-1, block_rows, slot_count),
        slot_mask(counts, slot_count).reshape(-1, block_rows, slot_count),
    )

    def one_block(portion):
        stored = edge_setup(
            portion[0], portion[1], portion[2], row_table, radial_weight, filter_weight
        )
        return edge_sums(stored, slot_count)

    return lax.map(one_block, pieces).reshape(atom_count, -1)


def atom_backward(
    indices, distances, counts, row_table, radial_weight, filter_weight, grad_message, early
):
    atom_count, slot_count = indices.shape
    block_rows = min(128, atom_count)
    pieces = (
        indices.reshape(-1, block_rows, slot_count),
        distances.reshape(-1, block_rows, slot_count),
        slot_mask(counts, slot_count).reshape(-1, block_rows, slot_count),
        grad_message.reshape(-1, block_rows, grad_message.shape[1]),
    )
    initial = (
        jnp.zeros(row_table.shape, jnp.float32),
        jnp.zeros(radial_weight.shape, jnp.float32),
        jnp.zeros(filter_weight.shape, jnp.float32),
    )

    steps = doubling_steps(("gy", "gx", "rep"))
    block_count = pieces[0].shape[0]
    per_block = -(-len(steps) // block_count)
    totals = initial
    for block in range(block_count):
        portion = tuple(piece[block] for piece in pieces)
        stored = edge_setup(
            portion[0], portion[1], portion[2], row_table, radial_weight, filter_weight
        )
        totals = edge_backward(stored, portion[0], filter_weight, portion[3], totals)
        for step in steps[block * per_block : (block + 1) * per_block]:
            early = doubling_step(early, step)
        totals, early = lax.optimization_barrier((totals, early))
    return totals, early


def probe_block(
    totals,
    indices,
    distances,
    cotangent,
    row_table,
    probe_radial,
    probe_filter,
    read_weight,
    final_weight,
):
    grad_table, grad_radial, grad_filter, grad_read, grad_final = totals
    stored = edge_setup(
        indices,
        distances,
        jnp.ones(indices.shape, jnp.float32),
        row_table,
        probe_radial,
        probe_filter,
    )
    packed = edge_sums(stored, indices.shape[1]).astype(jnp.bfloat16)
    read_pre = jnp.dot(packed, read_weight, preferred_element_type=jnp.float32)
    grad_final = grad_final + jnp.sum(cotangent[:, None] * shifted_plus(read_pre), axis=0)
    grad_inner = (cotangent[:, None] * final_weight[None, :] * jax.nn.sigmoid(read_pre)).astype(
        jnp.bfloat16
    )
    grad_read = grad_read + contract_rows(packed, grad_inner)
    grad_feats = contract_cols(grad_inner, read_weight)
    edge_totals = edge_backward(
        stored, indices, probe_filter, grad_feats, (grad_table, grad_radial, grad_filter)
    )
    return edge_totals + (grad_read, grad_final)


def interaction_head(atom_feats, kinds, species_gain, proj_input):
    onehot = (kinds[:, None] == jnp.arange(species_gain.shape[0], dtype=jnp.int32)[None, :]).astype(
        jnp.float32
    )
    gains = jnp.dot(onehot, species_gain, precision=lax.Precision.HIGHEST)
    scaled = (atom_feats.astype(jnp.float32) * gains).astype(jnp.bfloat16)
    projected = jnp.dot(scaled, proj_input, preferred_element_type=jnp.float32).astype(jnp.bfloat16)
    return (onehot, gains, scaled, projected)


def interaction_tail(atom_feats, message, mix_first, mix_second, proj_probe):
    packed_msg = message.astype(jnp.bfloat16)
    mix_pre = jnp.dot(packed_msg, mix_first, preferred_element_type=jnp.float32)
    activation = shifted_plus(mix_pre).astype(jnp.bfloat16)
    updated = (
        atom_feats.astype(jnp.float32)
        + jnp.dot(activation, mix_second, preferred_element_type=jnp.float32)
    ).astype(jnp.bfloat16)
    probe_proj = jnp.dot(updated, proj_probe, preferred_element_type=jnp.float32).astype(
        jnp.bfloat16
    )
    return (packed_msg, mix_pre, activation, updated, probe_proj)


def tail_backward(
    grad_proj, packed_msg, mix_pre, activation, updated, mix_first, mix_second, proj_probe
):
    grad_packed = grad_proj.astype(jnp.bfloat16)
    grad_proj_probe = contract_rows(updated, grad_packed)
    grad_updated = contract_cols(grad_packed, proj_probe)
    grad_upd_packed = grad_updated.astype(jnp.bfloat16)
    grad_mix_second = contract_rows(activation, grad_upd_packed)
    grad_mix_pre = (contract_cols(grad_upd_packed, mix_second) * jax.nn.sigmoid(mix_pre)).astype(
        jnp.bfloat16
    )
    grad_mix_first = contract_rows(packed_msg, grad_mix_pre)
    grad_message = contract_cols(grad_mix_pre, mix_first)
    return (grad_updated, grad_message, grad_proj_probe, grad_mix_second, grad_mix_first)


def head_backward(grad_proj, grad_updated, atom_feats, onehot, gains, scaled, proj_input):
    grad_packed = grad_proj.astype(jnp.bfloat16)
    grad_proj_input = contract_rows(scaled, grad_packed)
    grad_scaled = contract_cols(grad_packed, proj_input)
    d_features = grad_updated + grad_scaled * gains
    grad_gain = lax.dot_general(
        onehot,
        grad_scaled * atom_feats.astype(jnp.float32),
        (((0,), (0,)), ((), ())),
        precision=lax.Precision.HIGHEST,
    )
    return (d_features, grad_proj_input, grad_gain)


def add_rows(base, send_rows, returned):
    return base.at[send_rows.reshape(-1)].add(returned.reshape(-1, returned.shape[-1]))


def grid_of(blocks):
    empty = jnp.zeros((1,) + blocks.shape[1:], blocks.dtype)
    return jnp.concatenate([blocks[:4], empty, blocks[4:]], axis=0).reshape(
        (3, 3) + blocks.shape[1:]
    )


def blocks_of(layout):
    flat_grid = layout.reshape((9,) + layout.shape[2:])
    return jnp.concatenate([flat_grid[:4], flat_grid[5:]], axis=0)


def ghost_rows(blocks):
    layout = grid_of(blocks)
    padded = with_halo(layout, (("gx", 0), ("gy", 1)), 1)
    arrived = padded[0::2, 0::2]
    return blocks_of(arrived)


def ghost_grads(blocks):
    layout = grid_of(blocks)
    padded = with_halo(layout.astype(jnp.bfloat16), (("gx", 0), ("gy", 1)), 1).astype(layout.dtype)
    arrived = padded[0::2, 0::2]
    return blocks_of(arrived)


def per_device(
    features,
    species,
    atom_nbr,
    atom_nbr_count,
    atom_dist,
    send_list,
    probe_nbr,
    probe_dist,
    probe_count,
    d_density,
    species_gain,
    proj_input,
    atom_radial,
    atom_filter,
    mix_first,
    mix_second,
    proj_probe,
    probe_radial,
    probe_filter,
    read_weight,
    final_weight,
):
    atom_feats = features[0, 0, 0]
    atom_count = atom_feats.shape[0]
    feature_width = atom_feats.shape[1]
    send_rows = send_list[0, 0, 0]
    tile_nbr = atom_nbr[0, 0, 0]
    tile_dist = atom_dist[0, 0, 0]
    tile_counts = atom_nbr_count[0, 0, 0]
    onehot, gains, scaled, projected = interaction_head(
        atom_feats, species[0, 0, 0], species_gain, proj_input
    )
    row_table = jnp.concatenate(
        [projected, ghost_rows(projected[send_rows]).reshape(-1, feature_width)], axis=0
    )
    message = atom_messages(tile_nbr, tile_dist, tile_counts, row_table, atom_radial, atom_filter)
    packed_msg, mix_pre, activation, updated, probe_proj = interaction_tail(
        atom_feats, message, mix_first, mix_second, proj_probe
    )
    probe_table = jnp.concatenate(
        [probe_proj, ghost_rows(probe_proj[send_rows]).reshape(-1, feature_width)], axis=0
    )
    probe_ids = probe_nbr[0, 0, 0]
    probe_far = probe_dist[0, 0, 0]
    cotangents = d_density[0, 0, 0]
    block_rows = min(128, probe_ids.shape[0])
    active = probe_count[0, 0, 0]
    positions = jnp.arange(probe_ids.shape[0], dtype=jnp.int32)
    masked = cotangents * (positions < active).astype(jnp.float32)
    pieces = (
        probe_ids.reshape(-1, block_rows, probe_ids.shape[1]),
        probe_far.reshape(-1, block_rows, probe_far.shape[1]),
        masked.reshape(-1, block_rows),
    )
    initial = (
        jnp.zeros(probe_table.shape, jnp.float32),
        jnp.zeros(probe_radial.shape, jnp.float32),
        jnp.zeros(probe_filter.shape, jnp.float32),
        jnp.zeros(read_weight.shape, jnp.float32),
        jnp.zeros(final_weight.shape, jnp.float32),
    )

    def probe_turn(totals, portion):
        return (
            probe_block(
                totals,
                portion[0],
                portion[1],
                portion[2],
                probe_table,
                probe_radial,
                probe_filter,
                read_weight,
                final_weight,
            ),
            None,
        )

    grad_ptable, grad_pradial, grad_pfilter, grad_read, grad_final = lax.scan(
        probe_turn, initial, pieces
    )[0]
    probe_part = jnp.concatenate(
        [
            grad_pfilter.reshape(-1),
            grad_read.reshape(-1),
            grad_pradial.reshape(-1),
            grad_final.reshape(-1),
        ]
    )
    returned_probe = ghost_grads(
        grad_ptable[atom_count:].reshape(send_rows.shape + (feature_width,))
    )
    grad_q = add_rows(grad_ptable[:atom_count], send_rows, returned_probe)
    grad_updated, grad_message, grad_proj_probe, grad_mix_second, grad_mix_first = tail_backward(
        grad_q, packed_msg, mix_pre, activation, updated, mix_first, mix_second, proj_probe
    )
    tail_part = jnp.concatenate(
        [grad_mix_first.reshape(-1), grad_mix_second.reshape(-1), grad_proj_probe.reshape(-1)]
    )
    (grad_atable, grad_aradial, grad_afilter), early_sums = atom_backward(
        tile_nbr,
        tile_dist,
        tile_counts,
        row_table,
        atom_radial,
        atom_filter,
        grad_message,
        jnp.concatenate([probe_part, tail_part]),
    )
    returned_atom = ghost_grads(
        grad_atable[atom_count:].reshape(send_rows.shape + (feature_width,))
    )
    grad_u = add_rows(grad_atable[:atom_count], send_rows, returned_atom)
    d_features, grad_proj_input, grad_gain = head_backward(
        grad_u, grad_updated, atom_feats, onehot, gains, scaled, proj_input
    )
    atom_part = jnp.concatenate(
        [
            grad_afilter.reshape(-1),
            grad_proj_input.reshape(-1),
            grad_aradial.reshape(-1),
            grad_gain.reshape(-1),
        ]
    )
    atom_sums = summed_everywhere(atom_part, ("gy", "gx", "rep"))
    probe_sums = early_sums[: probe_part.shape[0]]
    tail_sums = early_sums[probe_part.shape[0] :]
    square = feature_width * feature_width
    radial = probe_radial.shape[0] * feature_width
    grad_square = jnp.concatenate(
        [
            probe_sums[: 2 * square],
            atom_sums[:square],
            atom_sums[square : 2 * square],
            tail_sums,
        ]
    ).reshape(7, feature_width, feature_width)
    grad_radial = jnp.concatenate(
        [probe_sums[2 * square : 2 * square + radial], atom_sums[2 * square : 2 * square + radial]]
    ).reshape(2, -1, feature_width)
    grad_vector = jnp.concatenate(
        [probe_sums[2 * square + radial :], atom_sums[2 * square + radial :]]
    ).reshape(-1, feature_width)
    return (d_features[None, None, None], grad_square, grad_radial, grad_vector)


def solution(mesh):
    in_specs = (
        P("rep", "gx", "gy", None, None),
        P("rep", "gx", "gy", None),
        P("rep", "gx", "gy", None, None),
        P("rep", "gx", "gy", None),
        P("rep", "gx", "gy", None, None),
        P("rep", "gx", "gy", None, None),
        P("rep", "gx", "gy", None, None),
        P("rep", "gx", "gy", None, None),
        P("rep", "gx", "gy"),
        P("rep", "gx", "gy", None),
        P(),
        P(),
        P(),
        P(),
        P(),
        P(),
        P(),
        P(),
        P(),
        P(),
        P(),
    )
    out_specs = (P("rep", "gx", "gy", None, None), P(), P(), P())
    return jax.shard_map(
        per_device, mesh=mesh, in_specs=in_specs, out_specs=out_specs, check_vma=False
    )
```

```python
import math

import jax
import jax.numpy as jnp
from jax import lax
from jax.sharding import PartitionSpec as P

cutoff_radius = 4.0


def with_halo(block, sides, width):
    for axis, dim in sides:
        count = lax.axis_size(axis)
        forward = [(i, i + 1) for i in range(count - 1)]
        forward.append((count - 1, 0))
        backward = [(target, source) for source, target in forward]
        low = lax.ppermute(
            lax.slice_in_dim(block, block.shape[dim] - width, None, axis=dim), axis, forward
        )
        high = lax.ppermute(lax.slice_in_dim(block, 0, width, axis=dim), axis, backward)
        block = jnp.concatenate([low, block, high], axis=dim)
    return block


def doubling_steps(axes):
    steps = []
    for axis in axes:
        stride = 1
        while stride < lax.axis_size(axis):
            steps.append((axis, stride))
            stride *= 2
    return steps


def doubling_step(values, step):
    axis, stride = step
    pairs = [(index, index ^ stride) for index in range(lax.axis_size(axis))]
    return values + lax.ppermute(values, axis, pairs)


def summed_everywhere(values, axes):
    for axis in axes:
        count = lax.axis_size(axis)
        stride = 1
        while stride < count:
            pairs = [(index, index ^ stride) for index in range(count)]
            values = values + lax.ppermute(values, axis, pairs)
            stride *= 2
    return values


def shifted_plus(values):
    return jax.nn.softplus(values) - math.log(2.0)


def contract_rows(former, latter):
    return lax.dot_general(
        former, latter, (((0,), (0,)), ((), ())), preferred_element_type=jnp.float32
    )


def contract_cols(former, latter):
    return lax.dot_general(
        former, latter, (((1,), (1,)), ((), ())), preferred_element_type=jnp.float32
    )


def one_hot_rows(indices, row_count):
    flat = indices.reshape(-1)
    return (flat[:, None] == jnp.arange(row_count, dtype=jnp.int32)[None, :]).astype(jnp.bfloat16)


def scatter_rows(indices, row_count, values):
    flat = indices.reshape(-1)
    spread = (jnp.arange(row_count, dtype=jnp.int32)[:, None] == flat[None, :]).astype(jnp.bfloat16)
    return jnp.dot(spread, values.astype(jnp.bfloat16), preferred_element_type=jnp.float32)


def edge_setup(
    indices, distances, live_mask, row_table, radial_weight, filter_weight, kept=None
):
    flat_dist = distances.reshape(-1)
    spacing = cutoff_radius / (radial_weight.shape[0] - 1)
    centers = jnp.arange(radial_weight.shape[0], dtype=jnp.float32) * spacing
    scaled = (flat_dist[None, :] - centers[:, None]) / spacing
    expansion = jnp.exp(-scaled * scaled).astype(jnp.bfloat16)
    pre_act = contract_rows(expansion, radial_weight)
    hidden = shifted_plus(pre_act).astype(jnp.bfloat16)
    envelope = 0.5 * (jnp.cos(math.pi * flat_dist / cutoff_radius) + 1.0) * live_mask.reshape(-1)
    if kept is not None:
        return (expansion, pre_act, hidden, envelope, kept[1], kept[0].astype(jnp.float32), None)
    filters = jnp.dot(hidden, filter_weight, preferred_element_type=jnp.float32) * envelope[:, None]
    selector = one_hot_rows(indices, row_table.shape[0])
    gathered = jnp.dot(selector, row_table, preferred_element_type=jnp.float32)
    return (expansion, pre_act, hidden, envelope, filters, gathered, selector)


def edge_sums(stored, slot_count):
    filters = stored[4]
    gathered = stored[5]
    terms = (gathered * filters).reshape(-1, slot_count, filters.shape[1])
    return jnp.sum(terms, axis=1)


def edge_backward(stored, indices, filter_weight, grad_message, totals):
    expansion, pre_act, hidden, envelope, filters, gathered, selector = stored
    grad_table, grad_radial, grad_filter = totals
    feature_width = grad_message.shape[1]
    spread = jnp.broadcast_to(
        grad_message[:, None, :], (grad_message.shape[0], indices.shape[1], feature_width)
    ).reshape(-1, feature_width)
    grad_table = grad_table + scatter_rows(indices, grad_table.shape[0], spread * filters)
    grad_out = (spread * gathered * envelope[:, None]).astype(jnp.bfloat16)
    grad_filter = grad_filter + contract_rows(hidden, grad_out)
    grad_pre = (contract_cols(grad_out, filter_weight) * jax.nn.sigmoid(pre_act)).astype(
        jnp.bfloat16
    )
    grad_radial = grad_radial + jnp.dot(expansion, grad_pre, preferred_element_type=jnp.float32)
    return (grad_table, grad_radial, grad_filter)


def slot_mask(counts, slot_count):
    return (jnp.arange(slot_count, dtype=jnp.int32)[None, :] < counts[:, None]).astype(jnp.float32)


def atom_messages(indices, distances, counts, row_table, radial_weight, filter_weight):
    atom_count, slot_count = indices.shape
    block_rows = min(128, atom_count)
    pieces = (
        indices.reshape(-1, block_rows, slot_count),
        distances.reshape(-1, block_rows, slot_count),
        slot_mask(counts, slot_count).reshape(-1, block_rows, slot_count),
    )

    def one_block(portion):
        stored = edge_setup(
            portion[0], portion[1], portion[2], row_table, radial_weight, filter_weight
        )
        return (edge_sums(stored, slot_count), (stored[5].astype(jnp.bfloat16), stored[4]))

    sums, kept = lax.map(one_block, pieces)
    return (sums.reshape(atom_count, -1), kept)


def atom_backward(
    indices, distances, counts, row_table, radial_weight, filter_weight, grad_message, early, kept
):
    atom_count, slot_count = indices.shape
    block_rows = min(128, atom_count)
    pieces = (
        indices.reshape(-1, block_rows, slot_count),
        distances.reshape(-1, block_rows, slot_count),
        slot_mask(counts, slot_count).reshape(-1, block_rows, slot_count),
        grad_message.reshape(-1, block_rows, grad_message.shape[1]),
    )
    initial = (
        jnp.zeros(row_table.shape, jnp.float32),
        jnp.zeros(radial_weight.shape, jnp.float32),
        jnp.zeros(filter_weight.shape, jnp.float32),
    )

    steps = doubling_steps(("gy", "gx", "rep"))
    block_count = pieces[0].shape[0]
    per_block = -(-len(steps) // block_count)
    totals = initial
    for block in range(block_count):
        portion = tuple(piece[block] for piece in pieces)
        stored = edge_setup(
            portion[0],
            portion[1],
            portion[2],
            row_table,
            radial_weight,
            filter_weight,
            (kept[0][block], kept[1][block]),
        )
        totals = edge_backward(stored, portion[0], filter_weight, portion[3], totals)
        for step in steps[block * per_block : (block + 1) * per_block]:
            early = doubling_step(early, step)
        totals, early = lax.optimization_barrier((totals, early))
    return totals, early


def probe_block(
    totals,
    indices,
    distances,
    cotangent,
    row_table,
    probe_radial,
    probe_filter,
    read_weight,
    final_weight,
):
    grad_table, grad_radial, grad_filter, grad_read, grad_final = totals
    stored = edge_setup(
        indices,
        distances,
        jnp.ones(indices.shape, jnp.float32),
        row_table,
        probe_radial,
        probe_filter,
    )
    packed = edge_sums(stored, indices.shape[1]).astype(jnp.bfloat16)
    read_pre = jnp.dot(packed, read_weight, preferred_element_type=jnp.float32)
    grad_final = grad_final + jnp.sum(cotangent[:, None] * shifted_plus(read_pre), axis=0)
    grad_inner = (cotangent[:, None] * final_weight[None, :] * jax.nn.sigmoid(read_pre)).astype(
        jnp.bfloat16
    )
    grad_read = grad_read + contract_rows(packed, grad_inner)
    grad_feats = contract_cols(grad_inner, read_weight)
    edge_totals = edge_backward(
        stored, indices, probe_filter, grad_feats, (grad_table, grad_radial, grad_filter)
    )
    return edge_totals + (grad_read, grad_final)


def interaction_head(atom_feats, kinds, species_gain, proj_input):
    onehot = (kinds[:, None] == jnp.arange(species_gain.shape[0], dtype=jnp.int32)[None, :]).astype(
        jnp.float32
    )
    gains = jnp.dot(onehot, species_gain, precision=lax.Precision.HIGHEST)
    scaled = (atom_feats.astype(jnp.float32) * gains).astype(jnp.bfloat16)
    projected = jnp.dot(scaled, proj_input, preferred_element_type=jnp.float32).astype(jnp.bfloat16)
    return (onehot, gains, scaled, projected)


def interaction_tail(atom_feats, message, mix_first, mix_second, proj_probe):
    packed_msg = message.astype(jnp.bfloat16)
    mix_pre = jnp.dot(packed_msg, mix_first, preferred_element_type=jnp.float32)
    activation = shifted_plus(mix_pre).astype(jnp.bfloat16)
    updated = (
        atom_feats.astype(jnp.float32)
        + jnp.dot(activation, mix_second, preferred_element_type=jnp.float32)
    ).astype(jnp.bfloat16)
    probe_proj = jnp.dot(updated, proj_probe, preferred_element_type=jnp.float32).astype(
        jnp.bfloat16
    )
    return (packed_msg, mix_pre, activation, updated, probe_proj)


def tail_backward(
    grad_proj, packed_msg, mix_pre, activation, updated, mix_first, mix_second, proj_probe
):
    grad_packed = grad_proj.astype(jnp.bfloat16)
    grad_proj_probe = contract_rows(updated, grad_packed)
    grad_updated = contract_cols(grad_packed, proj_probe)
    grad_upd_packed = grad_updated.astype(jnp.bfloat16)
    grad_mix_second = contract_rows(activation, grad_upd_packed)
    grad_mix_pre = (contract_cols(grad_upd_packed, mix_second) * jax.nn.sigmoid(mix_pre)).astype(
        jnp.bfloat16
    )
    grad_mix_first = contract_rows(packed_msg, grad_mix_pre)
    grad_message = contract_cols(grad_mix_pre, mix_first)
    return (grad_updated, grad_message, grad_proj_probe, grad_mix_second, grad_mix_first)


def head_backward(grad_proj, grad_updated, atom_feats, onehot, gains, scaled, proj_input):
    grad_packed = grad_proj.astype(jnp.bfloat16)
    grad_proj_input = contract_rows(scaled, grad_packed)
    grad_scaled = contract_cols(grad_packed, proj_input)
    d_features = grad_updated + grad_scaled * gains
    grad_gain = lax.dot_general(
        onehot,
        grad_scaled * atom_feats.astype(jnp.float32),
        (((0,), (0,)), ((), ())),
        precision=lax.Precision.HIGHEST,
    )
    return (d_features, grad_proj_input, grad_gain)


def add_rows(base, send_rows, returned):
    return base.at[send_rows.reshape(-1)].add(returned.reshape(-1, returned.shape[-1]))


def grid_of(blocks):
    empty = jnp.zeros((1,) + blocks.shape[1:], blocks.dtype)
    return jnp.concatenate([blocks[:4], empty, blocks[4:]], axis=0).reshape(
        (3, 3) + blocks.shape[1:]
    )


def blocks_of(layout):
    flat_grid = layout.reshape((9,) + layout.shape[2:])
    return jnp.concatenate([flat_grid[:4], flat_grid[5:]], axis=0)


def ghost_rows(blocks):
    layout = grid_of(blocks)
    padded = with_halo(layout, (("gx", 0), ("gy", 1)), 1)
    arrived = padded[0::2, 0::2]
    return blocks_of(arrived)


def ghost_grads(blocks):
    layout = grid_of(blocks)
    padded = with_halo(layout.astype(jnp.bfloat16), (("gx", 0), ("gy", 1)), 1).astype(layout.dtype)
    arrived = padded[0::2, 0::2]
    return blocks_of(arrived)


def per_device(
    features,
    species,
    atom_nbr,
    atom_nbr_count,
    atom_dist,
    send_list,
    probe_nbr,
    probe_dist,
    probe_count,
    d_density,
    species_gain,
    proj_input,
    atom_radial,
    atom_filter,
    mix_first,
    mix_second,
    proj_probe,
    probe_radial,
    probe_filter,
    read_weight,
    final_weight,
):
    atom_feats = features[0, 0, 0]
    atom_count = atom_feats.shape[0]
    feature_width = atom_feats.shape[1]
    send_rows = send_list[0, 0, 0]
    tile_nbr = atom_nbr[0, 0, 0]
    tile_dist = atom_dist[0, 0, 0]
    tile_counts = atom_nbr_count[0, 0, 0]
    onehot, gains, scaled, projected = interaction_head(
        atom_feats, species[0, 0, 0], species_gain, proj_input
    )
    row_table = jnp.concatenate(
        [projected, ghost_rows(projected[send_rows]).reshape(-1, feature_width)], axis=0
    )
    message, atom_kept = atom_messages(
        tile_nbr, tile_dist, tile_counts, row_table, atom_radial, atom_filter
    )
    packed_msg, mix_pre, activation, updated, probe_proj = interaction_tail(
        atom_feats, message, mix_first, mix_second, proj_probe
    )
    probe_table = jnp.concatenate(
        [probe_proj, ghost_rows(probe_proj[send_rows]).reshape(-1, feature_width)], axis=0
    )
    probe_ids = probe_nbr[0, 0, 0]
    probe_far = probe_dist[0, 0, 0]
    cotangents = d_density[0, 0, 0]
    block_rows = min(128, probe_ids.shape[0])
    active = probe_count[0, 0, 0]
    positions = jnp.arange(probe_ids.shape[0], dtype=jnp.int32)
    masked = cotangents * (positions < active).astype(jnp.float32)
    pieces = (
        probe_ids.reshape(-1, block_rows, probe_ids.shape[1]),
        probe_far.reshape(-1, block_rows, probe_far.shape[1]),
        masked.reshape(-1, block_rows),
    )
    initial = (
        jnp.zeros(probe_table.shape, jnp.float32),
        jnp.zeros(probe_radial.shape, jnp.float32),
        jnp.zeros(probe_filter.shape, jnp.float32),
        jnp.zeros(read_weight.shape, jnp.float32),
        jnp.zeros(final_weight.shape, jnp.float32),
    )

    def probe_turn(totals, portion):
        return (
            probe_block(
                totals,
                portion[0],
                portion[1],
                portion[2],
                probe_table,
                probe_radial,
                probe_filter,
                read_weight,
                final_weight,
            ),
            None,
        )

    grad_ptable, grad_pradial, grad_pfilter, grad_read, grad_final = lax.scan(
        probe_turn, initial, pieces
    )[0]
    probe_part = jnp.concatenate(
        [
            grad_pfilter.reshape(-1),
            grad_read.reshape(-1),
            grad_pradial.reshape(-1),
            grad_final.reshape(-1),
        ]
    )
    returned_probe = ghost_grads(
        grad_ptable[atom_count:].reshape(send_rows.shape + (feature_width,))
    )
    grad_q = add_rows(grad_ptable[:atom_count], send_rows, returned_probe)
    grad_updated, grad_message, grad_proj_probe, grad_mix_second, grad_mix_first = tail_backward(
        grad_q, packed_msg, mix_pre, activation, updated, mix_first, mix_second, proj_probe
    )
    tail_part = jnp.concatenate(
        [grad_mix_first.reshape(-1), grad_mix_second.reshape(-1), grad_proj_probe.reshape(-1)]
    )
    (grad_atable, grad_aradial, grad_afilter), early_sums = atom_backward(
        tile_nbr,
        tile_dist,
        tile_counts,
        row_table,
        atom_radial,
        atom_filter,
        grad_message,
        jnp.concatenate([probe_part, tail_part]),
        atom_kept,
    )
    returned_atom = ghost_grads(
        grad_atable[atom_count:].reshape(send_rows.shape + (feature_width,))
    )
    grad_u = add_rows(grad_atable[:atom_count], send_rows, returned_atom)
    d_features, grad_proj_input, grad_gain = head_backward(
        grad_u, grad_updated, atom_feats, onehot, gains, scaled, proj_input
    )
    atom_part = jnp.concatenate(
        [
            grad_afilter.reshape(-1),
            grad_proj_input.reshape(-1),
            grad_aradial.reshape(-1),
            grad_gain.reshape(-1),
        ]
    )
    atom_sums = summed_everywhere(atom_part, ("gy", "gx", "rep"))
    probe_sums = early_sums[: probe_part.shape[0]]
    tail_sums = early_sums[probe_part.shape[0] :]
    square = feature_width * feature_width
    radial = probe_radial.shape[0] * feature_width
    grad_square = jnp.concatenate(
        [
            probe_sums[: 2 * square],
            atom_sums[:square],
            atom_sums[square : 2 * square],
            tail_sums,
        ]
    ).reshape(7, feature_width, feature_width)
    grad_radial = jnp.concatenate(
        [probe_sums[2 * square : 2 * square + radial], atom_sums[2 * square : 2 * square + radial]]
    ).reshape(2, -1, feature_width)
    grad_vector = jnp.concatenate(
        [probe_sums[2 * square + radial :], atom_sums[2 * square + radial :]]
    ).reshape(-1, feature_width)
    return (d_features[None, None, None], grad_square, grad_radial, grad_vector)


def solution(mesh):
    in_specs = (
        P("rep", "gx", "gy", None, None),
        P("rep", "gx", "gy", None),
        P("rep", "gx", "gy", None, None),
        P("rep", "gx", "gy", None),
        P("rep", "gx", "gy", None, None),
        P("rep", "gx", "gy", None, None),
        P("rep", "gx", "gy", None, None),
        P("rep", "gx", "gy", None, None),
        P("rep", "gx", "gy"),
        P("rep", "gx", "gy", None),
        P(),
        P(),
        P(),
        P(),
        P(),
        P(),
        P(),
        P(),
        P(),
        P(),
        P(),
    )
    out_specs = (P("rep", "gx", "gy", None, None), P(), P(), P())
    return jax.shard_map(
        per_device, mesh=mesh, in_specs=in_specs, out_specs=out_specs, check_vma=False
    )
```

```python
import math

import jax
import jax.numpy as jnp
from jax import lax
from jax.sharding import PartitionSpec as P

cutoff_radius = 4.0


def with_halo(block, sides, width):
    for axis, dim in sides:
        count = lax.axis_size(axis)
        forward = [(i, i + 1) for i in range(count - 1)]
        forward.append((count - 1, 0))
        backward = [(target, source) for source, target in forward]
        low = lax.ppermute(
            lax.slice_in_dim(block, block.shape[dim] - width, None, axis=dim), axis, forward
        )
        high = lax.ppermute(lax.slice_in_dim(block, 0, width, axis=dim), axis, backward)
        block = jnp.concatenate([low, block, high], axis=dim)
    return block


def doubling_steps(axes):
    steps = []
    for axis in axes:
        stride = 1
        while stride < lax.axis_size(axis):
            steps.append((axis, stride))
            stride *= 2
    return steps


def doubling_step(values, step):
    axis, stride = step
    pairs = [(index, index ^ stride) for index in range(lax.axis_size(axis))]
    return values + lax.ppermute(values, axis, pairs)


def summed_everywhere(values, axes):
    for axis in axes:
        count = lax.axis_size(axis)
        stride = 1
        while stride < count:
            pairs = [(index, index ^ stride) for index in range(count)]
            values = values + lax.ppermute(values, axis, pairs)
            stride *= 2
    return values


def shifted_plus(values):
    return jax.nn.softplus(values) - math.log(2.0)


def contract_rows(former, latter):
    return lax.dot_general(
        former, latter, (((0,), (0,)), ((), ())), preferred_element_type=jnp.float32
    )


def contract_cols(former, latter):
    return lax.dot_general(
        former, latter, (((1,), (1,)), ((), ())), preferred_element_type=jnp.float32
    )


def one_hot_rows(indices, row_count):
    flat = indices.reshape(-1)
    return (flat[:, None] == jnp.arange(row_count, dtype=jnp.int32)[None, :]).astype(jnp.bfloat16)


def scatter_rows(indices, row_count, values):
    flat = indices.reshape(-1)
    spread = (jnp.arange(row_count, dtype=jnp.int32)[:, None] == flat[None, :]).astype(jnp.bfloat16)
    return jnp.dot(spread, values.astype(jnp.bfloat16), preferred_element_type=jnp.float32)


def edge_setup(
    indices, distances, live_mask, row_table, radial_weight, filter_weight, kept=None
):
    flat_dist = distances.reshape(-1)
    spacing = cutoff_radius / (radial_weight.shape[0] - 1)
    centers = jnp.arange(radial_weight.shape[0], dtype=jnp.float32) * spacing
    scaled = (flat_dist[None, :] - centers[:, None]) / spacing
    expansion = jnp.exp(-scaled * scaled).astype(jnp.bfloat16)
    pre_act = contract_rows(expansion, radial_weight)
    hidden = shifted_plus(pre_act).astype(jnp.bfloat16)
    envelope = 0.5 * (jnp.cos(math.pi * flat_dist / cutoff_radius) + 1.0) * live_mask.reshape(-1)
    if kept is not None:
        return (expansion, pre_act, hidden, envelope, kept[1], kept[0].astype(jnp.float32), None)
    filters = jnp.dot(hidden, filter_weight, preferred_element_type=jnp.float32) * envelope[:, None]
    selector = one_hot_rows(indices, row_table.shape[0])
    gathered = jnp.dot(selector, row_table, preferred_element_type=jnp.bfloat16)
    return (expansion, pre_act, hidden, envelope, filters, gathered.astype(jnp.float32), selector)


def edge_sums(stored, slot_count):
    filters = stored[4]
    gathered = stored[5]
    terms = (gathered * filters).reshape(-1, slot_count, filters.shape[1])
    return jnp.sum(terms, axis=1)


def edge_backward(stored, indices, filter_weight, grad_message, totals):
    expansion, pre_act, hidden, envelope, filters, gathered, selector = stored
    grad_table, grad_radial, grad_filter = totals
    feature_width = grad_message.shape[1]
    spread = jnp.broadcast_to(
        grad_message[:, None, :], (grad_message.shape[0], indices.shape[1], feature_width)
    ).reshape(-1, feature_width)
    grad_table = grad_table + scatter_rows(indices, grad_table.shape[0], spread * filters)
    grad_out = (spread * gathered * envelope[:, None]).astype(jnp.bfloat16)
    grad_filter = grad_filter + contract_rows(hidden, grad_out)
    grad_pre = (contract_cols(grad_out, filter_weight) * jax.nn.sigmoid(pre_act)).astype(
        jnp.bfloat16
    )
    grad_radial = grad_radial + jnp.dot(expansion, grad_pre, preferred_element_type=jnp.float32)
    return (grad_table, grad_radial, grad_filter)


def slot_mask(counts, slot_count):
    return (jnp.arange(slot_count, dtype=jnp.int32)[None, :] < counts[:, None]).astype(jnp.float32)


def atom_messages(indices, distances, counts, row_table, radial_weight, filter_weight):
    atom_count, slot_count = indices.shape
    block_rows = min(128, atom_count)
    pieces = (
        indices.reshape(-1, block_rows, slot_count),
        distances.reshape(-1, block_rows, slot_count),
        slot_mask(counts, slot_count).reshape(-1, block_rows, slot_count),
    )

    def one_block(portion):
        stored = edge_setup(
            portion[0], portion[1], portion[2], row_table, radial_weight, filter_weight
        )
        return (edge_sums(stored, slot_count), (stored[5].astype(jnp.bfloat16), stored[4]))

    sums, kept = lax.map(one_block, pieces)
    return (sums.reshape(atom_count, -1), kept)


def atom_backward(
    indices, distances, counts, row_table, radial_weight, filter_weight, grad_message, early, kept
):
    atom_count, slot_count = indices.shape
    block_rows = min(128, atom_count)
    pieces = (
        indices.reshape(-1, block_rows, slot_count),
        distances.reshape(-1, block_rows, slot_count),
        slot_mask(counts, slot_count).reshape(-1, block_rows, slot_count),
        grad_message.reshape(-1, block_rows, grad_message.shape[1]),
    )
    initial = (
        jnp.zeros(row_table.shape, jnp.float32),
        jnp.zeros(radial_weight.shape, jnp.float32),
        jnp.zeros(filter_weight.shape, jnp.float32),
    )

    steps = doubling_steps(("gy", "gx", "rep"))
    block_count = pieces[0].shape[0]
    per_block = -(-len(steps) // block_count)
    totals = initial
    for block in range(block_count):
        portion = tuple(piece[block] for piece in pieces)
        stored = edge_setup(
            portion[0],
            portion[1],
            portion[2],
            row_table,
            radial_weight,
            filter_weight,
            (kept[0][block], kept[1][block]),
        )
        totals = edge_backward(stored, portion[0], filter_weight, portion[3], totals)
        for step in steps[block * per_block : (block + 1) * per_block]:
            early = doubling_step(early, step)
        totals, early = lax.optimization_barrier((totals, early))
    return totals, early


def probe_block(
    totals,
    indices,
    distances,
    cotangent,
    row_table,
    probe_radial,
    probe_filter,
    read_weight,
    final_weight,
):
    grad_table, grad_radial, grad_filter, grad_read, grad_final = totals
    stored = edge_setup(
        indices,
        distances,
        jnp.ones(indices.shape, jnp.float32),
        row_table,
        probe_radial,
        probe_filter,
    )
    packed = edge_sums(stored, indices.shape[1]).astype(jnp.bfloat16)
    read_pre = jnp.dot(packed, read_weight, preferred_element_type=jnp.float32)
    grad_final = grad_final + jnp.sum(cotangent[:, None] * shifted_plus(read_pre), axis=0)
    grad_inner = (cotangent[:, None] * final_weight[None, :] * jax.nn.sigmoid(read_pre)).astype(
        jnp.bfloat16
    )
    grad_read = grad_read + contract_rows(packed, grad_inner)
    grad_feats = contract_cols(grad_inner, read_weight)
    edge_totals = edge_backward(
        stored, indices, probe_filter, grad_feats, (grad_table, grad_radial, grad_filter)
    )
    return edge_totals + (grad_read, grad_final)


def interaction_head(atom_feats, kinds, species_gain, proj_input):
    onehot = (kinds[:, None] == jnp.arange(species_gain.shape[0], dtype=jnp.int32)[None, :]).astype(
        jnp.float32
    )
    gains = jnp.dot(onehot, species_gain, precision=lax.Precision.HIGHEST)
    scaled = (atom_feats.astype(jnp.float32) * gains).astype(jnp.bfloat16)
    projected = jnp.dot(scaled, proj_input, preferred_element_type=jnp.float32).astype(jnp.bfloat16)
    return (onehot, gains, scaled, projected)


def interaction_tail(atom_feats, message, mix_first, mix_second, proj_probe):
    packed_msg = message.astype(jnp.bfloat16)
    mix_pre = jnp.dot(packed_msg, mix_first, preferred_element_type=jnp.float32)
    activation = shifted_plus(mix_pre).astype(jnp.bfloat16)
    updated = (
        atom_feats.astype(jnp.float32)
        + jnp.dot(activation, mix_second, preferred_element_type=jnp.float32)
    ).astype(jnp.bfloat16)
    probe_proj = jnp.dot(updated, proj_probe, preferred_element_type=jnp.float32).astype(
        jnp.bfloat16
    )
    return (packed_msg, mix_pre, activation, updated, probe_proj)


def tail_backward(
    grad_proj, packed_msg, mix_pre, activation, updated, mix_first, mix_second, proj_probe
):
    grad_packed = grad_proj.astype(jnp.bfloat16)
    grad_proj_probe = contract_rows(updated, grad_packed)
    grad_updated = contract_cols(grad_packed, proj_probe)
    grad_upd_packed = grad_updated.astype(jnp.bfloat16)
    grad_mix_second = contract_rows(activation, grad_upd_packed)
    grad_mix_pre = (contract_cols(grad_upd_packed, mix_second) * jax.nn.sigmoid(mix_pre)).astype(
        jnp.bfloat16
    )
    grad_mix_first = contract_rows(packed_msg, grad_mix_pre)
    grad_message = contract_cols(grad_mix_pre, mix_first)
    return (grad_updated, grad_message, grad_proj_probe, grad_mix_second, grad_mix_first)


def head_backward(grad_proj, grad_updated, atom_feats, onehot, gains, scaled, proj_input):
    grad_packed = grad_proj.astype(jnp.bfloat16)
    grad_proj_input = contract_rows(scaled, grad_packed)
    grad_scaled = contract_cols(grad_packed, proj_input)
    d_features = grad_updated + grad_scaled * gains
    grad_gain = lax.dot_general(
        onehot,
        grad_scaled * atom_feats.astype(jnp.float32),
        (((0,), (0,)), ((), ())),
        precision=lax.Precision.HIGHEST,
    )
    return (d_features, grad_proj_input, grad_gain)


def add_rows(base, send_rows, returned):
    return base.at[send_rows.reshape(-1)].add(returned.reshape(-1, returned.shape[-1]))


def grid_of(blocks):
    empty = jnp.zeros((1,) + blocks.shape[1:], blocks.dtype)
    return jnp.concatenate([blocks[:4], empty, blocks[4:]], axis=0).reshape(
        (3, 3) + blocks.shape[1:]
    )


def blocks_of(layout):
    flat_grid = layout.reshape((9,) + layout.shape[2:])
    return jnp.concatenate([flat_grid[:4], flat_grid[5:]], axis=0)


def ghost_rows(blocks):
    layout = grid_of(blocks)
    padded = with_halo(layout, (("gx", 0), ("gy", 1)), 1)
    arrived = padded[0::2, 0::2]
    return blocks_of(arrived)


def ghost_grads(blocks):
    layout = grid_of(blocks)
    padded = with_halo(layout.astype(jnp.bfloat16), (("gx", 0), ("gy", 1)), 1).astype(layout.dtype)
    arrived = padded[0::2, 0::2]
    return blocks_of(arrived)


def per_device(
    features,
    species,
    atom_nbr,
    atom_nbr_count,
    atom_dist,
    send_list,
    probe_nbr,
    probe_dist,
    probe_count,
    d_density,
    species_gain,
    proj_input,
    atom_radial,
    atom_filter,
    mix_first,
    mix_second,
    proj_probe,
    probe_radial,
    probe_filter,
    read_weight,
    final_weight,
):
    atom_feats = features[0, 0, 0]
    atom_count = atom_feats.shape[0]
    feature_width = atom_feats.shape[1]
    send_rows = send_list[0, 0, 0]
    tile_nbr = atom_nbr[0, 0, 0]
    tile_dist = atom_dist[0, 0, 0]
    tile_counts = atom_nbr_count[0, 0, 0]
    onehot, gains, scaled, projected = interaction_head(
        atom_feats, species[0, 0, 0], species_gain, proj_input
    )
    row_table = jnp.concatenate(
        [projected, ghost_rows(projected[send_rows]).reshape(-1, feature_width)], axis=0
    )
    message, atom_kept = atom_messages(
        tile_nbr, tile_dist, tile_counts, row_table, atom_radial, atom_filter
    )
    packed_msg, mix_pre, activation, updated, probe_proj = interaction_tail(
        atom_feats, message, mix_first, mix_second, proj_probe
    )
    probe_table = jnp.concatenate(
        [probe_proj, ghost_rows(probe_proj[send_rows]).reshape(-1, feature_width)], axis=0
    )
    probe_ids = probe_nbr[0, 0, 0]
    probe_far = probe_dist[0, 0, 0]
    cotangents = d_density[0, 0, 0]
    block_rows = min(128, probe_ids.shape[0])
    active = probe_count[0, 0, 0]
    positions = jnp.arange(probe_ids.shape[0], dtype=jnp.int32)
    masked = cotangents * (positions < active).astype(jnp.float32)
    pieces = (
        probe_ids.reshape(-1, block_rows, probe_ids.shape[1]),
        probe_far.reshape(-1, block_rows, probe_far.shape[1]),
        masked.reshape(-1, block_rows),
    )
    initial = (
        jnp.zeros(probe_table.shape, jnp.float32),
        jnp.zeros(probe_radial.shape, jnp.float32),
        jnp.zeros(probe_filter.shape, jnp.float32),
        jnp.zeros(read_weight.shape, jnp.float32),
        jnp.zeros(final_weight.shape, jnp.float32),
    )

    def probe_turn(totals, portion):
        return (
            probe_block(
                totals,
                portion[0],
                portion[1],
                portion[2],
                probe_table,
                probe_radial,
                probe_filter,
                read_weight,
                final_weight,
            ),
            None,
        )

    grad_ptable, grad_pradial, grad_pfilter, grad_read, grad_final = lax.scan(
        probe_turn, initial, pieces
    )[0]
    probe_part = jnp.concatenate(
        [
            grad_pfilter.reshape(-1),
            grad_read.reshape(-1),
            grad_pradial.reshape(-1),
            grad_final.reshape(-1),
        ]
    )
    returned_probe = ghost_grads(
        grad_ptable[atom_count:].reshape(send_rows.shape + (feature_width,))
    )
    grad_q = add_rows(grad_ptable[:atom_count], send_rows, returned_probe)
    grad_updated, grad_message, grad_proj_probe, grad_mix_second, grad_mix_first = tail_backward(
        grad_q, packed_msg, mix_pre, activation, updated, mix_first, mix_second, proj_probe
    )
    tail_part = jnp.concatenate(
        [grad_mix_first.reshape(-1), grad_mix_second.reshape(-1), grad_proj_probe.reshape(-1)]
    )
    (grad_atable, grad_aradial, grad_afilter), early_sums = atom_backward(
        tile_nbr,
        tile_dist,
        tile_counts,
        row_table,
        atom_radial,
        atom_filter,
        grad_message,
        jnp.concatenate([probe_part, tail_part]),
        atom_kept,
    )
    returned_atom = ghost_grads(
        grad_atable[atom_count:].reshape(send_rows.shape + (feature_width,))
    )
    grad_u = add_rows(grad_atable[:atom_count], send_rows, returned_atom)
    d_features, grad_proj_input, grad_gain = head_backward(
        grad_u, grad_updated, atom_feats, onehot, gains, scaled, proj_input
    )
    atom_part = jnp.concatenate(
        [
            grad_afilter.reshape(-1),
            grad_proj_input.reshape(-1),
            grad_aradial.reshape(-1),
            grad_gain.reshape(-1),
        ]
    )
    atom_sums = summed_everywhere(atom_part, ("gy", "gx", "rep"))
    probe_sums = early_sums[: probe_part.shape[0]]
    tail_sums = early_sums[probe_part.shape[0] :]
    square = feature_width * feature_width
    radial = probe_radial.shape[0] * feature_width
    grad_square = jnp.concatenate(
        [
            probe_sums[: 2 * square],
            atom_sums[:square],
            atom_sums[square : 2 * square],
            tail_sums,
        ]
    ).reshape(7, feature_width, feature_width)
    grad_radial = jnp.concatenate(
        [probe_sums[2 * square : 2 * square + radial], atom_sums[2 * square : 2 * square + radial]]
    ).reshape(2, -1, feature_width)
    grad_vector = jnp.concatenate(
        [probe_sums[2 * square + radial :], atom_sums[2 * square + radial :]]
    ).reshape(-1, feature_width)
    return (d_features[None, None, None], grad_square, grad_radial, grad_vector)


def solution(mesh):
    in_specs = (
        P("rep", "gx", "gy", None, None),
        P("rep", "gx", "gy", None),
        P("rep", "gx", "gy", None, None),
        P("rep", "gx", "gy", None),
        P("rep", "gx", "gy", None, None),
        P("rep", "gx", "gy", None, None),
        P("rep", "gx", "gy", None, None),
        P("rep", "gx", "gy", None, None),
        P("rep", "gx", "gy"),
        P("rep", "gx", "gy", None),
        P(),
        P(),
        P(),
        P(),
        P(),
        P(),
        P(),
        P(),
        P(),
        P(),
        P(),
    )
    out_specs = (P("rep", "gx", "gy", None, None), P(), P(), P())
    return jax.shard_map(
        per_device, mesh=mesh, in_specs=in_specs, out_specs=out_specs, check_vma=False
    )
```

```python
import math

import jax
import jax.numpy as jnp
from jax import lax
from jax.sharding import PartitionSpec as P

cutoff_radius = 4.0


def with_halo(block, sides, width):
    for axis, dim in sides:
        count = lax.axis_size(axis)
        forward = [(i, i + 1) for i in range(count - 1)]
        forward.append((count - 1, 0))
        backward = [(target, source) for source, target in forward]
        low = lax.ppermute(
            lax.slice_in_dim(block, block.shape[dim] - width, None, axis=dim), axis, forward
        )
        high = lax.ppermute(lax.slice_in_dim(block, 0, width, axis=dim), axis, backward)
        block = jnp.concatenate([low, block, high], axis=dim)
    return block


def doubling_steps(axes):
    steps = []
    for axis in axes:
        stride = 1
        while stride < lax.axis_size(axis):
            steps.append((axis, stride))
            stride *= 2
    return steps


def doubling_step(values, step):
    axis, stride = step
    pairs = [(index, index ^ stride) for index in range(lax.axis_size(axis))]
    return values + lax.ppermute(values, axis, pairs)


def summed_everywhere(values, axes):
    for axis in axes:
        count = lax.axis_size(axis)
        stride = 1
        while stride < count:
            pairs = [(index, index ^ stride) for index in range(count)]
            values = values + lax.ppermute(values, axis, pairs)
            stride *= 2
    return values


def shifted_plus(values):
    return jax.nn.softplus(values) - math.log(2.0)


def contract_rows(former, latter):
    return lax.dot_general(
        former, latter, (((0,), (0,)), ((), ())), preferred_element_type=jnp.float32
    )


def contract_cols(former, latter):
    return lax.dot_general(
        former, latter, (((1,), (1,)), ((), ())), preferred_element_type=jnp.float32
    )


def one_hot_rows(indices, row_count):
    flat = indices.reshape(-1)
    return (flat[:, None] == jnp.arange(row_count, dtype=jnp.int32)[None, :]).astype(jnp.bfloat16)


def scatter_rows(indices, row_count, values):
    flat = indices.reshape(-1)
    spread = (jnp.arange(row_count, dtype=jnp.int32)[:, None] == flat[None, :]).astype(jnp.bfloat16)
    return jnp.dot(spread, values.astype(jnp.bfloat16), preferred_element_type=jnp.float32)


def edge_setup(
    indices, distances, live_mask, row_table, radial_weight, filter_weight, kept=None
):
    flat_dist = distances.reshape(-1)
    spacing = cutoff_radius / (radial_weight.shape[0] - 1)
    centers = jnp.arange(radial_weight.shape[0], dtype=jnp.float32) * spacing
    scaled = (flat_dist[None, :] - centers[:, None]) / spacing
    expansion = jnp.exp(-scaled * scaled).astype(jnp.bfloat16)
    pre_act = contract_rows(expansion, radial_weight)
    hidden = shifted_plus(pre_act).astype(jnp.bfloat16)
    envelope = 0.5 * (jnp.cos(math.pi * flat_dist / cutoff_radius) + 1.0) * live_mask.reshape(-1)
    if kept is not None:
        return (expansion, pre_act, hidden, envelope, kept[1], kept[0].astype(jnp.float32), None)
    filters = jnp.dot(hidden, filter_weight, preferred_element_type=jnp.float32) * envelope[:, None]
    selector = one_hot_rows(indices, row_table.shape[0])
    gathered = jnp.dot(selector, row_table, preferred_element_type=jnp.float32)
    return (expansion, pre_act, hidden, envelope, filters, gathered, selector)


def edge_sums(stored, slot_count):
    filters = stored[4]
    gathered = stored[5]
    terms = (gathered * filters).reshape(-1, slot_count, filters.shape[1])
    return jnp.sum(terms, axis=1)


def edge_backward(stored, indices, filter_weight, grad_message, totals):
    expansion, pre_act, hidden, envelope, filters, gathered, selector = stored
    grad_table, grad_radial, grad_filter = totals
    feature_width = grad_message.shape[1]
    spread = jnp.broadcast_to(
        grad_message[:, None, :], (grad_message.shape[0], indices.shape[1], feature_width)
    ).reshape(-1, feature_width)
    grad_table = grad_table + scatter_rows(indices, grad_table.shape[0], spread * filters)
    grad_out = (spread * gathered * envelope[:, None]).astype(jnp.bfloat16)
    grad_filter = grad_filter + contract_rows(hidden, grad_out)
    grad_pre = (contract_cols(grad_out, filter_weight) * jax.nn.sigmoid(pre_act)).astype(
        jnp.bfloat16
    )
    grad_radial = grad_radial + jnp.dot(expansion, grad_pre, preferred_element_type=jnp.float32)
    return (grad_table, grad_radial, grad_filter)


def slot_mask(counts, slot_count):
    return (jnp.arange(slot_count, dtype=jnp.int32)[None, :] < counts[:, None]).astype(jnp.float32)


def atom_messages(indices, distances, counts, row_table, radial_weight, filter_weight):
    atom_count, slot_count = indices.shape
    block_rows = min(128, atom_count)
    pieces = (
        indices.reshape(-1, block_rows, slot_count),
        distances.reshape(-1, block_rows, slot_count),
        slot_mask(counts, slot_count).reshape(-1, block_rows, slot_count),
    )

    def one_block(portion):
        stored = edge_setup(
            portion[0], portion[1], portion[2], row_table, radial_weight, filter_weight
        )
        return (edge_sums(stored, slot_count), (stored[5].astype(jnp.bfloat16), stored[4]))

    sums, kept = lax.map(one_block, pieces)
    return (sums.reshape(atom_count, -1), kept)


def atom_backward(
    indices, distances, counts, row_table, radial_weight, filter_weight, grad_message, early, kept
):
    atom_count, slot_count = indices.shape
    block_rows = min(128, atom_count)
    pieces = (
        indices.reshape(-1, block_rows, slot_count),
        distances.reshape(-1, block_rows, slot_count),
        slot_mask(counts, slot_count).reshape(-1, block_rows, slot_count),
        grad_message.reshape(-1, block_rows, grad_message.shape[1]),
    )
    initial = (
        jnp.zeros(row_table.shape, jnp.float32),
        jnp.zeros(radial_weight.shape, jnp.float32),
        jnp.zeros(filter_weight.shape, jnp.float32),
    )

    steps = doubling_steps(("gy", "gx", "rep"))
    block_count = pieces[0].shape[0]
    per_block = -(-len(steps) // block_count)
    totals = initial
    for block in range(block_count):
        portion = tuple(piece[block] for piece in pieces)
        stored = edge_setup(
            portion[0],
            portion[1],
            portion[2],
            row_table,
            radial_weight,
            filter_weight,
            (kept[0][block], kept[1][block]),
        )
        totals = edge_backward(stored, portion[0], filter_weight, portion[3], totals)
        for step in steps[block * per_block : (block + 1) * per_block]:
            early = doubling_step(early, step)
        totals, early = lax.optimization_barrier((totals, early))
    return totals, early


def probe_block(
    totals,
    indices,
    distances,
    cotangent,
    row_table,
    probe_radial,
    probe_filter,
    read_weight,
    final_weight,
):
    grad_table, grad_radial, grad_filter, grad_read, grad_final = totals
    stored = edge_setup(
        indices,
        distances,
        jnp.ones(indices.shape, jnp.float32),
        row_table,
        probe_radial,
        probe_filter,
    )
    packed = edge_sums(stored, indices.shape[1]).astype(jnp.bfloat16)
    read_pre = jnp.dot(packed, read_weight, preferred_element_type=jnp.float32)
    grad_final = grad_final + jnp.sum(cotangent[:, None] * shifted_plus(read_pre), axis=0)
    grad_inner = (cotangent[:, None] * final_weight[None, :] * jax.nn.sigmoid(read_pre)).astype(
        jnp.bfloat16
    )
    grad_read = grad_read + contract_rows(packed, grad_inner)
    grad_feats = contract_cols(grad_inner, read_weight)
    edge_totals = edge_backward(
        stored, indices, probe_filter, grad_feats, (grad_table, grad_radial, grad_filter)
    )
    return edge_totals + (grad_read, grad_final)


def interaction_head(atom_feats, kinds, species_gain, proj_input):
    onehot = (kinds[:, None] == jnp.arange(species_gain.shape[0], dtype=jnp.int32)[None, :]).astype(
        jnp.float32
    )
    gains = jnp.dot(onehot, species_gain, precision=lax.Precision.HIGHEST)
    scaled = (atom_feats.astype(jnp.float32) * gains).astype(jnp.bfloat16)
    projected = jnp.dot(scaled, proj_input, preferred_element_type=jnp.float32).astype(jnp.bfloat16)
    return (onehot, gains, scaled, projected)


def interaction_tail(atom_feats, message, mix_first, mix_second, proj_probe):
    packed_msg = message.astype(jnp.bfloat16)
    mix_pre = jnp.dot(packed_msg, mix_first, preferred_element_type=jnp.float32)
    activation = shifted_plus(mix_pre).astype(jnp.bfloat16)
    updated = (
        atom_feats.astype(jnp.float32)
        + jnp.dot(activation, mix_second, preferred_element_type=jnp.float32)
    ).astype(jnp.bfloat16)
    probe_proj = jnp.dot(updated, proj_probe, preferred_element_type=jnp.float32).astype(
        jnp.bfloat16
    )
    return (packed_msg, mix_pre, activation, updated, probe_proj)


def tail_backward(
    grad_proj, packed_msg, mix_pre, activation, updated, mix_first, mix_second, proj_probe
):
    grad_packed = grad_proj.astype(jnp.bfloat16)
    grad_proj_probe = contract_rows(updated, grad_packed)
    grad_updated = contract_cols(grad_packed, proj_probe)
    grad_upd_packed = grad_updated.astype(jnp.bfloat16)
    grad_mix_second = contract_rows(activation, grad_upd_packed)
    grad_mix_pre = (contract_cols(grad_upd_packed, mix_second) * jax.nn.sigmoid(mix_pre)).astype(
        jnp.bfloat16
    )
    grad_mix_first = contract_rows(packed_msg, grad_mix_pre)
    grad_message = contract_cols(grad_mix_pre, mix_first)
    return (grad_updated, grad_message, grad_proj_probe, grad_mix_second, grad_mix_first)


def head_backward(grad_proj, grad_updated, atom_feats, onehot, gains, scaled, proj_input):
    grad_packed = grad_proj.astype(jnp.bfloat16)
    grad_proj_input = contract_rows(scaled, grad_packed)
    grad_scaled = contract_cols(grad_packed, proj_input)
    d_features = grad_updated + grad_scaled * gains
    grad_gain = lax.dot_general(
        onehot,
        grad_scaled * atom_feats.astype(jnp.float32),
        (((0,), (0,)), ((), ())),
        precision=lax.Precision.HIGHEST,
    )
    return (d_features, grad_proj_input, grad_gain)


def add_rows(base, send_rows, returned):
    return base.at[send_rows.reshape(-1)].add(returned.reshape(-1, returned.shape[-1]))


def grid_of(blocks):
    empty = jnp.zeros((1,) + blocks.shape[1:], blocks.dtype)
    return jnp.concatenate([blocks[:4], empty, blocks[4:]], axis=0).reshape(
        (3, 3) + blocks.shape[1:]
    )


def blocks_of(layout):
    flat_grid = layout.reshape((9,) + layout.shape[2:])
    return jnp.concatenate([flat_grid[:4], flat_grid[5:]], axis=0)


def ghost_rows(blocks):
    layout = grid_of(blocks)
    padded = with_halo(layout, (("gx", 0), ("gy", 1)), 1)
    arrived = padded[0::2, 0::2]
    return blocks_of(arrived)


def ghost_grads(blocks):
    layout = grid_of(blocks)
    padded = with_halo(layout.astype(jnp.bfloat16), (("gx", 0), ("gy", 1)), 1).astype(layout.dtype)
    arrived = padded[0::2, 0::2]
    return blocks_of(arrived)


def per_device(
    features,
    species,
    atom_nbr,
    atom_nbr_count,
    atom_dist,
    send_list,
    probe_nbr,
    probe_dist,
    probe_count,
    d_density,
    species_gain,
    proj_input,
    atom_radial,
    atom_filter,
    mix_first,
    mix_second,
    proj_probe,
    probe_radial,
    probe_filter,
    read_weight,
    final_weight,
):
    atom_feats = features[0, 0, 0]
    atom_count = atom_feats.shape[0]
    feature_width = atom_feats.shape[1]
    send_rows = send_list[0, 0, 0]
    tile_nbr = atom_nbr[0, 0, 0]
    tile_dist = atom_dist[0, 0, 0]
    tile_counts = atom_nbr_count[0, 0, 0]
    onehot, gains, scaled, projected = interaction_head(
        atom_feats, species[0, 0, 0], species_gain, proj_input
    )
    row_table = jnp.concatenate(
        [projected, ghost_rows(projected[send_rows]).reshape(-1, feature_width)], axis=0
    )
    message, atom_kept = atom_messages(
        tile_nbr, tile_dist, tile_counts, row_table, atom_radial, atom_filter
    )
    packed_msg, mix_pre, activation, updated, probe_proj = interaction_tail(
        atom_feats, message, mix_first, mix_second, proj_probe
    )
    probe_table = jnp.concatenate(
        [probe_proj, ghost_rows(probe_proj[send_rows]).reshape(-1, feature_width)], axis=0
    )
    probe_ids = probe_nbr[0, 0, 0]
    probe_far = probe_dist[0, 0, 0]
    cotangents = d_density[0, 0, 0]
    block_rows = min(128, probe_ids.shape[0])
    active = probe_count[0, 0, 0]
    positions = jnp.arange(probe_ids.shape[0], dtype=jnp.int32)
    masked = cotangents * (positions < active).astype(jnp.float32)
    pieces = (
        probe_ids.reshape(-1, block_rows, probe_ids.shape[1]),
        probe_far.reshape(-1, block_rows, probe_far.shape[1]),
        masked.reshape(-1, block_rows),
    )
    initial = (
        jnp.zeros(probe_table.shape, jnp.float32),
        jnp.zeros(probe_radial.shape, jnp.float32),
        jnp.zeros(probe_filter.shape, jnp.float32),
        jnp.zeros(read_weight.shape, jnp.float32),
        jnp.zeros(final_weight.shape, jnp.float32),
    )

    def probe_turn(totals, portion):
        return (
            probe_block(
                totals,
                portion[0],
                portion[1],
                portion[2],
                probe_table,
                probe_radial,
                probe_filter,
                read_weight,
                final_weight,
            ),
            None,
        )

    grad_ptable, grad_pradial, grad_pfilter, grad_read, grad_final = lax.scan(
        probe_turn, initial, pieces
    )[0]
    probe_part = jnp.concatenate(
        [
            grad_pfilter.reshape(-1),
            grad_read.reshape(-1),
            grad_pradial.reshape(-1),
            grad_final.reshape(-1),
        ]
    )
    returned_probe = ghost_grads(
        grad_ptable[atom_count:].reshape(send_rows.shape + (feature_width,))
    )
    grad_q = add_rows(grad_ptable[:atom_count], send_rows, returned_probe)
    grad_updated, grad_message, grad_proj_probe, grad_mix_second, grad_mix_first = tail_backward(
        grad_q, packed_msg, mix_pre, activation, updated, mix_first, mix_second, proj_probe
    )
    tail_part = jnp.concatenate(
        [grad_mix_first.reshape(-1), grad_mix_second.reshape(-1), grad_proj_probe.reshape(-1)]
    )
    (grad_atable, grad_aradial, grad_afilter), early_sums = atom_backward(
        tile_nbr,
        tile_dist,
        tile_counts,
        row_table,
        atom_radial,
        atom_filter,
        grad_message,
        jnp.concatenate([probe_part, tail_part]),
        atom_kept,
    )
    filter_sums = summed_everywhere(
        jnp.concatenate([grad_afilter.reshape(-1), grad_aradial.reshape(-1)]), ("gy", "gx", "rep")
    )
    returned_atom = ghost_grads(
        grad_atable[atom_count:].reshape(send_rows.shape + (feature_width,))
    )
    grad_u = add_rows(grad_atable[:atom_count], send_rows, returned_atom)
    d_features, grad_proj_input, grad_gain = head_backward(
        grad_u, grad_updated, atom_feats, onehot, gains, scaled, proj_input
    )
    input_sums = summed_everywhere(
        jnp.concatenate([grad_proj_input.reshape(-1), grad_gain.reshape(-1)]), ("gy", "gx", "rep")
    )
    square = feature_width * feature_width
    atom_sums = jnp.concatenate(
        [filter_sums[:square], input_sums[:square], filter_sums[square:], input_sums[square:]]
    )
    probe_sums = early_sums[: probe_part.shape[0]]
    tail_sums = early_sums[probe_part.shape[0] :]
    square = feature_width * feature_width
    radial = probe_radial.shape[0] * feature_width
    grad_square = jnp.concatenate(
        [
            probe_sums[: 2 * square],
            atom_sums[:square],
            atom_sums[square : 2 * square],
            tail_sums,
        ]
    ).reshape(7, feature_width, feature_width)
    grad_radial = jnp.concatenate(
        [probe_sums[2 * square : 2 * square + radial], atom_sums[2 * square : 2 * square + radial]]
    ).reshape(2, -1, feature_width)
    grad_vector = jnp.concatenate(
        [probe_sums[2 * square + radial :], atom_sums[2 * square + radial :]]
    ).reshape(-1, feature_width)
    return (d_features[None, None, None], grad_square, grad_radial, grad_vector)


def solution(mesh):
    in_specs = (
        P("rep", "gx", "gy", None, None),
        P("rep", "gx", "gy", None),
        P("rep", "gx", "gy", None, None),
        P("rep", "gx", "gy", None),
        P("rep", "gx", "gy", None, None),
        P("rep", "gx", "gy", None, None),
        P("rep", "gx", "gy", None, None),
        P("rep", "gx", "gy", None, None),
        P("rep", "gx", "gy"),
        P("rep", "gx", "gy", None),
        P(),
        P(),
        P(),
        P(),
        P(),
        P(),
        P(),
        P(),
        P(),
        P(),
        P(),
    )
    out_specs = (P("rep", "gx", "gy", None, None), P(), P(), P())
    return jax.shard_map(
        per_device, mesh=mesh, in_specs=in_specs, out_specs=out_specs, check_vma=False
    )
```
